128 devices in a mesh: section: 2 (over core), seq: 64 (over z, x, y).
Axes of the slice: x: 4, y: 4, z: 4, core: 2. Of those that a mesh axis runs over, the one named last changes fastest.
Arguments:
- patches: bfloat16 [32768, 1408], P('seq'), may hold values from -42 to 42
- image_grid: int32 [256, 2], P('seq'), may hold values from 2 to 52, as said below
- image_offsets: int32 [256], P('seq'), may hold values from 0 to 32736, as said below
- dest_positions: int32 [8192], replicated, may hold values from 0 to 16383, as said below
- text_embeds: bfloat16 [256, 64, 1408], P(None, 'seq'), may hold values from -42 to 42
- segment_ids: int32 [256, 64], replicated, may hold values from 0 to 3, as said below
- vision_qkv: bfloat16 [1408, 3, 1408], P(None, None, 'section'), may hold values from -0.15625 to 0.15625
- vision_out: bfloat16 [1408, 1408], P('section'), may hold values from -0.875 to 0.875
- projector: bfloat16 [4, 1408, 1408], P('section'), may hold values from -0.078125 to 0.078125
- decoder_q: bfloat16 [1408, 1408], P(None, 'section'), may hold values from -0.15625 to 0.15625
- decoder_kv: bfloat16 [1408, 2, 176], P(None, None, 'section'), may hold values from -0.15625 to 0.15625
- decoder_out: bfloat16 [1408, 1408], P('section'), may hold values from -0.875 to 0.875
Outputs:
- decoded: bfloat16 [256, 64, 1408], P(None, 'seq')
The draws below stay inside these ranges and needn't reach their ends.
Inputs may be any that keep to these rules, and one draw needn't show every extreme that they name: `image_grid`: patch rows and columns are even, columns are 8 or 16; the images of one index of seq lie back to back and cover exactly its 512 patches. `image_offsets`: each image's first patch; images are in order, back to back, the first of an index of seq at its first patch. `dest_positions`: the 128 merged rows of one index of seq go, in order, to 128 consecutive prompt positions; the ranges of different indices do not meet. `segment_ids`: never falls along prompt positions; every document number is used.
All inputs are finite; a program needn't handle non-finite values.
Results may differ from the reference program's by a relative error of at most 0.025.
Values may be sent and summed in bfloat16 or wider, within the bound.
No kernel may reach another device: no remote copies, remote signals or barrier semaphores. Data moves between devices by JAX's collectives and lax.ppermute only.
A program may use at most 128 MiB of HBM per device.

```python
import math
import jax
import jax.numpy as jnp
from jax import lax

D = 1408
HEADS = 16
HEAD = 88
KV_HEADS = 2
IMG_DEV = 4
P_DEV = 512
T_DEV = 256
DOCS = 4
M_DEV = 128
PATCHES = 32768
IMAGES = 256
M_TOTAL = 8192
PROMPT = 16384
N_SEQ = 64


def draw_floats(key, count):
    key_values, key_column, key_row = jax.random.split(key, 3)
    lowest = math.log(0.32)
    highest = math.log(3.2)
    column_scale = jnp.exp(jax.random.uniform(key_column, (D,), jnp.float32, lowest, highest))
    row_scale = jnp.exp(jax.random.uniform(key_row, (count, 1), jnp.float32, lowest, highest))
    values = jnp.clip(jax.random.normal(key_values, (count, D), jnp.float32), -4.0, 4.0)
    return 0.5 * values * column_scale[None, :] * row_scale


def draw_patches(key, part):
    return draw_floats(jax.random.fold_in(key, 3), PATCHES).astype(jnp.bfloat16)


def draw_text_embeds(key, part):
    return draw_floats(jax.random.fold_in(key, 5), PROMPT).reshape(T_DEV, PROMPT // T_DEV, D).astype(jnp.bfloat16)


def image_layout(key):
    base = jax.random.fold_in(key, 11)
    blocks = IMAGES // IMG_DEV
    units = P_DEV // 32

    def one_block(block_key, forced):
        key_cut, key_width = jax.random.split(block_key)
        cuts = jnp.sort(jax.random.permutation(key_cut, units - 1)[:IMG_DEV - 1].astype(jnp.int32) + 1)
        cuts = jnp.where(forced, jnp.arange(1, IMG_DEV, dtype=jnp.int32), cuts)
        bounds = jnp.concatenate([jnp.zeros((1,), jnp.int32), cuts, jnp.full((1,), units, jnp.int32)])
        counts = bounds[1:] - bounds[:-1]
        widths = 4 * jax.random.randint(key_width, (IMG_DEV,), 1, 3).astype(jnp.int32)
        fixed_widths = jnp.concatenate([jnp.full((IMG_DEV - 1,), 8, jnp.int32), jnp.full((1,), 4, jnp.int32)])
        widths = jnp.where(forced, fixed_widths, widths)
        heights = 8 * counts // widths
        return (2 * heights, 2 * widths, 32 * bounds[:-1])
    forced_flags = jnp.arange(blocks, dtype=jnp.int32) == 0
    heights, widths, starts = jax.vmap(one_block)(jax.random.split(base, blocks), forced_flags)
    starts = starts + (jnp.arange(blocks, dtype=jnp.int32) * P_DEV)[:, None]
    grid = jnp.stack([heights.reshape(-1), widths.reshape(-1)], 1).astype(jnp.int32)
    return (grid, starts.reshape(-1).astype(jnp.int32))


def draw_image_grid(key, part):
    return image_layout(key)[0]


def draw_image_offsets(key, part):
    return image_layout(key)[1]


def draw_dest_positions(key, part):
    key_order, key_gap = jax.random.split(jax.random.fold_in(key, 13))
    blocks = M_TOTAL // M_DEV
    spare = PROMPT - M_TOTAL
    order = jax.random.permutation(key_order, blocks)
    before = jnp.sort(jax.random.randint(key_gap, (blocks,), 0, spare + 1).astype(jnp.int32))
    run_starts = jnp.arange(blocks, dtype=jnp.int32) * M_DEV + before
    starts = jnp.zeros((blocks,), jnp.int32).at[order].set(run_starts)
    return (starts[:, None] + jnp.arange(M_DEV, dtype=jnp.int32)[None, :]).reshape(-1).astype(jnp.int32)


def draw_segment_ids(key, part):
    cuts = jnp.sort(jax.random.permutation(jax.random.fold_in(key, 17), PROMPT - 1)[:DOCS - 1].astype(jnp.int32) + 1)
    positions = jnp.arange(PROMPT, dtype=jnp.int32)
    labels = jnp.sum((positions[:, None] >= cuts[None, :]).astype(jnp.int32), 1)
    return labels.astype(jnp.int32).reshape(T_DEV, PROMPT // T_DEV)


def level_of(own_key, extent, pieces, low, largest):
    factor_of = 1.0
    for dim, shards_of in pieces:
        draws = jax.random.uniform(jax.random.fold_in(jax.random.fold_in(own_key, 6), dim), (shards_of,), jnp.float32, low / len(pieces), largest / len(pieces))
        factor_of = factor_of * jnp.repeat(jnp.exp(draws), extent[dim] // shards_of).reshape((-1,) + (1,) * (len(extent) - 1 - dim))
    return factor_of


def gaussian(key, extent, scale, most, pieces=(), kind=jnp.bfloat16):
    level = level_of(key, extent, pieces, -0.22, 0.18) if pieces else 1.0
    array = jax.random.normal(key, extent, jnp.float32) * scale * level
    return jnp.minimum(jnp.maximum(array, -most), most).astype(kind)


def setup_inputs(seed: int = 0) -> dict:
    key_of = jax.random.split(jax.random.key(seed), 13)
    return {
        "patches": draw_patches(jax.random.fold_in(key_of[12], 71), 0),
        "image_grid": draw_image_grid(jax.random.fold_in(key_of[12], 71), 0),
        "image_offsets": draw_image_offsets(jax.random.fold_in(key_of[12], 71), 0),
        "dest_positions": draw_dest_positions(jax.random.fold_in(key_of[12], 71), 0),
        "text_embeds": draw_text_embeds(jax.random.fold_in(key_of[12], 71), 0),
        "segment_ids": draw_segment_ids(jax.random.fold_in(key_of[12], 71), 0),
        "vision_qkv": gaussian(key_of[6], (D, 3, HEADS * HEAD), D ** -0.5, 0.15625, ((2, 2),)),
        "vision_out": gaussian(key_of[7], (HEADS * HEAD, D), (HEADS * HEAD // 32) ** -0.5, 0.875, ((0, 2),)),
        "projector": gaussian(key_of[8], (4, D, D), (4 * D) ** -0.5, 0.078125, ((0, 2),)),
        "decoder_q": gaussian(key_of[9], (D, HEADS * HEAD), D ** -0.5, 0.15625, ((1, 2),)),
        "decoder_kv": gaussian(key_of[10], (D, 2, KV_HEADS * HEAD), D ** -0.5, 0.15625, ((2, 2),)),
        "decoder_out": gaussian(key_of[11], (HEADS * HEAD, D), (HEADS * HEAD // 32) ** -0.5, 0.875, ((0, 2),)),
    }


def layer_norm(values):
    values = values.astype(jnp.float32)
    centred = values - lax.optimization_barrier(jnp.mean(values, -1, keepdims=True))
    return centred * lax.rsqrt(lax.optimization_barrier(jnp.mean(centred * centred, -1, keepdims=True)) + 1e-06)

def root_norm(values):
    values = values.astype(jnp.float32)
    return values * lax.rsqrt(lax.optimization_barrier(jnp.mean(values * values, -1, keepdims=True)) + 1e-06)

def merge_rows(grid, offsets, count):
    heights = grid[:, 0]
    widths = grid[:, 1]
    group_start = offsets // 4
    group_count = heights * widths // 4
    merged_ids = jnp.arange(count, dtype=jnp.int32)
    inside = ((merged_ids[:, None] >= group_start[None, :]) & (merged_ids[:, None] < (group_start + group_count)[None, :])).astype(jnp.int32)
    first_group = lax.optimization_barrier(jnp.sum(inside * group_start[None, :], 1))
    first_patch = lax.optimization_barrier(jnp.sum(inside * offsets[None, :], 1))
    row_width = lax.optimization_barrier(jnp.sum(inside * widths[None, :], 1))
    within = merged_ids - first_group
    groups_across = row_width // 2
    group_row = within // groups_across
    group_col = within % groups_across
    corner = first_patch + 2 * group_row * row_width + 2 * group_col
    return jnp.stack([corner, corner + 1, corner + row_width, corner + row_width + 1], 1).astype(jnp.int32)

def reference(patches, image_grid, image_offsets, dest_positions, text_embeds, segment_ids, vision_qkv, vision_out, projector, decoder_q, decoder_kv, decoder_out):
    scale = 3.0 / math.sqrt(HEAD)
    width = HEADS * HEAD
    qkv_matrix = vision_qkv.reshape(D, 3 * width)
    merge_matrix = projector.reshape(4 * D, D)

    def vision_block(block):
        patch_rows = lax.dynamic_slice_in_dim(patches, block * P_DEV, P_DEV, 0)
        grid = lax.dynamic_slice_in_dim(image_grid, block * IMG_DEV, IMG_DEV, 0)
        offsets = lax.dynamic_slice_in_dim(image_offsets, block * IMG_DEV, IMG_DEV, 0) - block * P_DEV
        normed = layer_norm(patch_rows).astype(jnp.bfloat16)
        mixed = jnp.dot(normed, qkv_matrix, preferred_element_type=jnp.float32).reshape(P_DEV, 3, HEADS, HEAD)
        queries = root_norm(mixed[:, 0]).astype(jnp.bfloat16)
        keys = root_norm(mixed[:, 1]).astype(jnp.bfloat16)
        values = mixed[:, 2].astype(jnp.bfloat16)
        image_of = lax.optimization_barrier(jnp.sum((jnp.arange(P_DEV, dtype=jnp.int32)[:, None] >= offsets[None, :]).astype(jnp.int32), 1))
        same = image_of[:, None] == image_of[None, :]
        scores = jnp.einsum('qhd,khd->hqk', queries.astype(jnp.float32), keys.astype(jnp.float32)) * scale
        weights = jnp.where(same[None], jnp.exp(scores), jnp.zeros_like(scores))
        totals = lax.optimization_barrier(jnp.sum(weights, -1))
        rounded = lax.optimization_barrier(weights.astype(jnp.bfloat16))
        mixed_values = jnp.einsum('hqk,khd->qhd', rounded.astype(jnp.float32), values.astype(jnp.float32))
        attended = (mixed_values / jnp.transpose(totals)[:, :, None]).astype(jnp.bfloat16).reshape(P_DEV, width)
        vision = (patch_rows.astype(jnp.float32) + jnp.dot(attended, vision_out, preferred_element_type=jnp.float32)).astype(jnp.bfloat16)
        picks = merge_rows(grid, offsets, M_DEV)
        merged = vision[picks.reshape(-1)].reshape(M_DEV, 4 * D)
        return jnp.dot(merged, merge_matrix, preferred_element_type=jnp.float32).astype(jnp.bfloat16)
    image_rows = lax.map(vision_block, jnp.arange(N_SEQ, dtype=jnp.int32)).reshape(M_TOTAL, D)
    prompt = text_embeds.reshape(PROMPT, D).at[dest_positions].set(image_rows)
    normed = root_norm(prompt).astype(jnp.bfloat16)
    group = HEADS // KV_HEADS
    queries = root_norm(jnp.dot(normed, decoder_q, preferred_element_type=jnp.float32).reshape(PROMPT, HEADS, HEAD)).astype(jnp.bfloat16)
    queries = queries.reshape(PROMPT, KV_HEADS, group, HEAD)
    paired = jnp.dot(normed, decoder_kv.reshape(D, 2 * KV_HEADS * HEAD), preferred_element_type=jnp.float32).reshape(PROMPT, 2, KV_HEADS, HEAD)
    keys = root_norm(paired[:, 0]).astype(jnp.bfloat16)
    values = paired[:, 1].astype(jnp.bfloat16)
    places = jnp.arange(PROMPT, dtype=jnp.int32)
    segments = segment_ids.reshape(PROMPT)
    block_rows = 128

    def text_block(first):
        query_rows = lax.dynamic_slice_in_dim(queries, first, block_rows, 0)
        query_places = first + jnp.arange(block_rows, dtype=jnp.int32)
        query_segments = lax.dynamic_slice_in_dim(segments, first, block_rows, 0)
        allowed = (places[None, :] <= query_places[:, None]) & (segments[None, :] == query_segments[:, None])
        scores = jnp.einsum('qkgd,lkd->qkgl', query_rows.astype(jnp.float32), keys.astype(jnp.float32)) * scale
        weights = jnp.where(allowed[:, None, None, :], jnp.exp(scores), jnp.zeros_like(scores))
        totals = lax.optimization_barrier(jnp.sum(weights, -1))
        rounded = lax.optimization_barrier(weights.astype(jnp.bfloat16))
        mixed_values = jnp.einsum('qkgl,lkd->qkgd', rounded.astype(jnp.float32), values.astype(jnp.float32))
        return (mixed_values / totals[..., None]).astype(jnp.bfloat16).reshape(block_rows, HEADS * HEAD)
    attended = lax.map(text_block, jnp.arange(PROMPT // block_rows, dtype=jnp.int32) * block_rows).reshape(PROMPT, HEADS * HEAD)
    decoded = (prompt.astype(jnp.float32) + jnp.dot(attended, decoder_out, preferred_element_type=jnp.float32)).astype(jnp.bfloat16)
    return decoded.reshape(T_DEV, N_SEQ, D)
```

```python
import math

import jax
import jax.numpy as jnp
from jax import lax
from jax.sharding import PartitionSpec as P

D = 1408
HEAD = 88
CHUNKS = 4


def layer_norm(values):
    values = values.astype(jnp.float32)
    centred = values - jnp.mean(values, -1, keepdims=True)
    return centred * lax.rsqrt(jnp.mean(centred * centred, -1, keepdims=True) + 1e-06)


def root_norm(values):
    values = values.astype(jnp.float32)
    return values * lax.rsqrt(jnp.mean(values * values, -1, keepdims=True) + 1e-06)


def merge_rows(grid, offsets, count):
    heights = grid[:, 0]
    widths = grid[:, 1]
    group_start = offsets // 4
    group_count = heights * widths // 4
    merged_ids = jnp.arange(count, dtype=jnp.int32)
    inside = (
        (merged_ids[:, None] >= group_start[None, :])
        & (merged_ids[:, None] < (group_start + group_count)[None, :])
    ).astype(jnp.int32)
    first_group = jnp.sum(inside * group_start[None, :], 1)
    first_patch = jnp.sum(inside * offsets[None, :], 1)
    row_width = jnp.sum(inside * widths[None, :], 1)
    within = merged_ids - first_group
    groups_across = row_width // 2
    group_row = within // groups_across
    group_col = within % groups_across
    corner = first_patch + 2 * group_row * row_width + 2 * group_col
    return jnp.stack([corner, corner + 1, corner + row_width, corner + row_width + 1], 1)


def swap(values):
    return lax.ppermute(values, "section", [(0, 1), (1, 0)])


def in_head_order(first, own, other, axis):
    return jnp.where(
        first, jnp.concatenate([own, other], axis), jnp.concatenate([other, own], axis)
    )


def body(
    patches,
    image_grid,
    image_offsets,
    dest_positions,
    text_embeds,
    segment_ids,
    vision_qkv,
    vision_out,
    projector,
    decoder_q,
    decoder_kv,
    decoder_out,
):
    section_index = lax.axis_index("section")
    seq_index = lax.axis_index("seq")
    seq_count = lax.axis_size("seq")
    first = section_index == 0
    scale = 3.0 / math.sqrt(HEAD)
    patch_count = patches.shape[0]
    local_heads = vision_out.shape[0] // HEAD
    merged_count = patch_count // 4

    vision_out_other = swap(vision_out)
    decoder_out_full = in_head_order(first, decoder_out, swap(decoder_out), 0)

    normed = layer_norm(patches).astype(jnp.bfloat16)
    mixed = jnp.dot(normed, vision_qkv.reshape(D, -1), preferred_element_type=jnp.float32).reshape(
        patch_count, 3, local_heads, HEAD
    )
    queries = root_norm(mixed[:, 0]).astype(jnp.bfloat16)
    keys = root_norm(mixed[:, 1]).astype(jnp.bfloat16)
    values = mixed[:, 2].astype(jnp.bfloat16)
    offsets = image_offsets - seq_index * patch_count
    image_of = jnp.sum(
        (jnp.arange(patch_count, dtype=jnp.int32)[:, None] >= offsets[None, :]).astype(jnp.int32), 1
    )
    scores = jnp.einsum("qhd,khd->hqk", queries, keys, preferred_element_type=jnp.float32) * scale
    same = (image_of[:, None] == image_of[None, :])[None]
    weights = jnp.where(same, jnp.exp(scores), jnp.zeros_like(scores))
    totals = jnp.sum(weights, -1)
    mixed_values = jnp.einsum(
        "hqk,khd->qhd", weights.astype(jnp.bfloat16), values, preferred_element_type=jnp.float32
    )
    attended = (
        (mixed_values / jnp.transpose(totals)[:, :, None])
        .astype(jnp.bfloat16)
        .reshape(patch_count, local_heads * HEAD)
    )
    picks = merge_rows(image_grid, offsets, merged_count)
    own_picks = lax.dynamic_slice_in_dim(picks, 2 * section_index, 2, 1).reshape(-1)
    other_picks = lax.dynamic_slice_in_dim(picks, 2 - 2 * section_index, 2, 1).reshape(-1)
    received_heads = swap(attended[other_picks])
    own_rows = jnp.concatenate([attended[own_picks], received_heads], 1)
    full_out = jnp.concatenate([vision_out, vision_out_other], 0)
    kept = (
        patches[own_picks].astype(jnp.float32)
        + jnp.dot(own_rows, full_out, preferred_element_type=jnp.float32)
    ).astype(jnp.bfloat16)
    merge_terms = jnp.dot(
        kept.reshape(merged_count, 2 * D),
        projector.reshape(2 * D, D),
        preferred_element_type=jnp.float32,
    )
    image_rows = (merge_terms + swap(merge_terms)).astype(jnp.bfloat16)

    per_peer = merged_count // seq_count
    run_starts = dest_positions.reshape(seq_count, merged_count)[:, 0]
    own_start = run_starts[seq_index]
    received = lax.all_to_all(
        jnp.roll(image_rows.reshape(per_peer, seq_count, image_rows.shape[1]), own_start, axis=1),
        "seq",
        split_axis=1,
        concat_axis=1,
        tiled=True,
    )
    slot_base = jnp.arange(per_peer, dtype=jnp.int32)[:, None] * seq_count
    landing = (
        run_starts[None, :] + slot_base + (seq_index - run_starts[None, :]) % seq_count
    ) // seq_count
    text_rows = text_embeds.shape[0]
    prompt = text_embeds.reshape(text_rows, D).at[landing.reshape(-1)].set(received.reshape(-1, D))
    text_normed = root_norm(prompt).astype(jnp.bfloat16)
    text_queries = root_norm(
        jnp.dot(text_normed, decoder_q, preferred_element_type=jnp.float32).reshape(
            text_rows, local_heads, HEAD
        )
    ).astype(jnp.bfloat16)
    paired = jnp.dot(
        text_normed, decoder_kv.reshape(D, -1), preferred_element_type=jnp.float32
    ).reshape(text_rows, 2, HEAD)
    key_rows = root_norm(paired[:, 0]).astype(jnp.bfloat16)
    value_rows = paired[:, 1].astype(jnp.bfloat16)
    shared = jnp.stack([key_rows, value_rows], 1)

    query_places = jnp.arange(text_rows, dtype=jnp.int32) * seq_count + seq_index
    query_segments = lax.dynamic_slice_in_dim(segment_ids, seq_index, 1, 1)[:, 0]
    step = text_rows // CHUNKS
    sums = jnp.zeros((text_rows, local_heads, HEAD), jnp.float32)
    totals = jnp.zeros((text_rows, local_heads), jnp.float32)
    for chunk in range(CHUNKS):
        low = chunk * step
        piece = lax.all_gather(shared[None, low : low + step], "seq", axis=0, tiled=True)
        piece = piece.reshape(seq_count * step, 2, HEAD)
        key_places = (
            jnp.arange(seq_count, dtype=jnp.int32)[:, None]
            + (low + jnp.arange(step, dtype=jnp.int32))[None, :] * seq_count
        ).reshape(-1)
        key_segments = jnp.transpose(segment_ids[low : low + step]).reshape(-1)
        chunk_queries = text_queries[low:]
        scores = (
            jnp.einsum("qgd,ld->qgl", chunk_queries, piece[:, 0], preferred_element_type=jnp.float32)
            * scale
        )
        allowed = (key_places[None, :] <= query_places[low:, None]) & (
            key_segments[None, :] == query_segments[low:, None]
        )
        weights = jnp.where(allowed[:, None, :], jnp.exp(scores), jnp.zeros_like(scores))
        totals = totals.at[low:].add(jnp.sum(weights, -1))
        sums = sums.at[low:].add(
            jnp.einsum(
                "qgl,ld->qgd",
                weights.astype(jnp.bfloat16),
                piece[:, 1],
                preferred_element_type=jnp.float32,
            )
        )
    attended_text = (sums / totals[..., None]).astype(jnp.bfloat16).reshape(text_rows, -1)
    all_heads = in_head_order(first, attended_text, swap(attended_text), 1)
    output_terms = jnp.dot(all_heads, decoder_out_full, preferred_element_type=jnp.float32)
    decoded = (prompt.astype(jnp.float32) + output_terms).astype(jnp.bfloat16)
    return decoded.reshape(text_rows, 1, D)


def solution(mesh):
    placed = (
        P("seq", None),
        P("seq", None),
        P("seq"),
        P(),
        P(None, "seq", None),
        P(),
        P(None, None, "section"),
        P("section", None),
        P("section", None, None),
        P(None, "section"),
        P(None, None, "section"),
        P("section", None),
    )
    return jax.shard_map(
        body, mesh=mesh, in_specs=placed, out_specs=P(None, "seq", None), check_vma=False
    )
```

```python
import math

import jax
import jax.numpy as jnp
from jax import lax
from jax.sharding import PartitionSpec as P

D = 1408
HEAD = 88


def layer_norm(values):
    values = values.astype(jnp.float32)
    centred = values - jnp.mean(values, -1, keepdims=True)
    return centred * lax.rsqrt(jnp.mean(centred * centred, -1, keepdims=True) + 1e-06)


def root_norm(values):
    values = values.astype(jnp.float32)
    return values * lax.rsqrt(jnp.mean(values * values, -1, keepdims=True) + 1e-06)


def merge_rows(grid, offsets, count):
    heights = grid[:, 0]
    widths = grid[:, 1]
    group_start = offsets // 4
    group_count = heights * widths // 4
    merged_ids = jnp.arange(count, dtype=jnp.int32)
    inside = (
        (merged_ids[:, None] >= group_start[None, :])
        & (merged_ids[:, None] < (group_start + group_count)[None, :])
    ).astype(jnp.int32)
    first_group = jnp.sum(inside * group_start[None, :], 1)
    first_patch = jnp.sum(inside * offsets[None, :], 1)
    row_width = jnp.sum(inside * widths[None, :], 1)
    within = merged_ids - first_group
    groups_across = row_width // 2
    group_row = within // groups_across
    group_col = within % groups_across
    corner = first_patch + 2 * group_row * row_width + 2 * group_col
    return jnp.stack([corner, corner + 1, corner + row_width, corner + row_width + 1], 1)


def swap(values):
    return lax.ppermute(values, "section", [(0, 1), (1, 0)])


def in_head_order(first, own, other, axis):
    return jnp.where(
        first, jnp.concatenate([own, other], axis), jnp.concatenate([other, own], axis)
    )


def body(
    patches,
    image_grid,
    image_offsets,
    dest_positions,
    text_embeds,
    segment_ids,
    vision_qkv,
    vision_out,
    projector,
    decoder_q,
    decoder_kv,
    decoder_out,
):
    section_index = lax.axis_index("section")
    seq_index = lax.axis_index("seq")
    seq_count = lax.axis_size("seq")
    first = section_index == 0
    scale = 3.0 / math.sqrt(HEAD)
    patch_count = patches.shape[0]
    local_heads = vision_out.shape[0] // HEAD
    merged_count = patch_count // 4

    vision_out_other = swap(vision_out)
    decoder_out_full = in_head_order(first, decoder_out, swap(decoder_out), 0)

    normed = layer_norm(patches).astype(jnp.bfloat16)
    mixed = jnp.dot(normed, vision_qkv.reshape(D, -1), preferred_element_type=jnp.float32).reshape(
        patch_count, 3, local_heads, HEAD
    )
    queries = root_norm(mixed[:, 0]).astype(jnp.bfloat16)
    keys = root_norm(mixed[:, 1]).astype(jnp.bfloat16)
    values = mixed[:, 2].astype(jnp.bfloat16)
    offsets = image_offsets - seq_index * patch_count
    image_of = jnp.sum(
        (jnp.arange(patch_count, dtype=jnp.int32)[:, None] >= offsets[None, :]).astype(jnp.int32), 1
    )
    scores = jnp.einsum("qhd,khd->hqk", queries, keys, preferred_element_type=jnp.float32) * scale
    same = (image_of[:, None] == image_of[None, :])[None]
    weights = jnp.where(same, jnp.exp(scores), jnp.zeros_like(scores))
    totals = jnp.sum(weights, -1)
    mixed_values = jnp.einsum(
        "hqk,khd->qhd", weights.astype(jnp.bfloat16), values, preferred_element_type=jnp.float32
    )
    attended = (
        (mixed_values / jnp.transpose(totals)[:, :, None])
        .astype(jnp.bfloat16)
        .reshape(patch_count, local_heads * HEAD)
    )
    picks = merge_rows(image_grid, offsets, merged_count)
    own_picks = lax.dynamic_slice_in_dim(picks, 2 * section_index, 2, 1).reshape(-1)
    other_picks = lax.dynamic_slice_in_dim(picks, 2 - 2 * section_index, 2, 1).reshape(-1)
    received_heads = swap(attended[other_picks])
    own_rows = jnp.concatenate([attended[own_picks], received_heads], 1)
    full_out = jnp.concatenate([vision_out, vision_out_other], 0)
    kept = (
        patches[own_picks].astype(jnp.float32)
        + jnp.dot(own_rows, full_out, preferred_element_type=jnp.float32)
    ).astype(jnp.bfloat16)
    merge_terms = jnp.dot(
        kept.reshape(merged_count, 2 * D),
        projector.reshape(2 * D, D),
        preferred_element_type=jnp.float32,
    )
    image_rows = (merge_terms + swap(merge_terms)).astype(jnp.bfloat16)

    per_peer = merged_count // seq_count
    run_starts = dest_positions.reshape(seq_count, merged_count)[:, 0]
    own_start = run_starts[seq_index]
    received = lax.all_to_all(
        jnp.roll(image_rows.reshape(per_peer, seq_count, image_rows.shape[1]), own_start, axis=1),
        "seq",
        split_axis=1,
        concat_axis=1,
        tiled=True,
    )
    slot_base = jnp.arange(per_peer, dtype=jnp.int32)[:, None] * seq_count
    landing = (
        run_starts[None, :] + slot_base + (seq_index - run_starts[None, :]) % seq_count
    ) // seq_count
    text_rows = text_embeds.shape[0]
    prompt = text_embeds.reshape(text_rows, D).at[landing.reshape(-1)].set(received.reshape(-1, D))
    text_normed = root_norm(prompt).astype(jnp.bfloat16)
    text_queries = root_norm(
        jnp.dot(text_normed, decoder_q, preferred_element_type=jnp.float32).reshape(
            text_rows, local_heads, HEAD
        )
    ).astype(jnp.bfloat16)
    paired = jnp.dot(
        text_normed, decoder_kv.reshape(D, -1), preferred_element_type=jnp.float32
    ).reshape(text_rows, 2, HEAD)
    key_rows = root_norm(paired[:, 0]).astype(jnp.bfloat16)
    value_rows = paired[:, 1].astype(jnp.bfloat16)
    shared = jnp.stack([key_rows, value_rows], 1)

    query_places = jnp.arange(text_rows, dtype=jnp.int32) * seq_count + seq_index
    query_segments = lax.dynamic_slice_in_dim(segment_ids, seq_index, 1, 1)[:, 0]
    text_queries = text_queries.reshape(text_rows, 1, local_heads, HEAD)
    start_state = (
        jnp.zeros((text_rows, 1, local_heads, HEAD), jnp.float32),
        jnp.zeros((text_rows, 1, local_heads), jnp.float32),
    )
    piece = lax.all_gather(shared.reshape(1, text_rows, 2, 1, HEAD), "seq", axis=0, tiled=True)
    shards = piece.shape[0]
    stride = math.gcd(shards, 8)
    blocks = shards // stride
    key_segments = jnp.transpose(segment_ids).reshape(blocks, stride * text_rows)
    shard_ids = jnp.arange(shards, dtype=jnp.int32)
    key_places = (
        jnp.arange(text_rows, dtype=jnp.int32)[None, :] * seq_count + shard_ids[:, None]
    ).reshape(blocks, stride * text_rows)
    grouped = piece.reshape(blocks, stride * text_rows, 2, 1, HEAD)

    def one_block(state, inputs):
        block_pair, block_places, block_segments = inputs
        scores = (
            jnp.einsum(
                "qkgd,lkd->qkgl", text_queries, block_pair[:, 0], preferred_element_type=jnp.float32
            )
            * scale
        )
        allowed = (block_places[None, :] <= query_places[:, None]) & (
            block_segments[None, :] == query_segments[:, None]
        )
        weights = jnp.where(allowed[:, None, None, :], jnp.exp(scores), jnp.zeros_like(scores))
        totals = state[1] + jnp.sum(weights, -1)
        sums = state[0] + jnp.einsum(
            "qkgl,lkd->qkgd",
            weights.astype(jnp.bfloat16),
            block_pair[:, 1],
            preferred_element_type=jnp.float32,
        )
        return ((sums, totals), None)

    result, unused = lax.scan(one_block, start_state, (grouped, key_places, key_segments))
    sums, totals = result
    attended_text = (sums / totals[..., None]).astype(jnp.bfloat16).reshape(text_rows, -1)
    all_heads = in_head_order(first, attended_text, swap(attended_text), 1)
    output_terms = jnp.dot(all_heads, decoder_out_full, preferred_element_type=jnp.float32)
    decoded = (prompt.astype(jnp.float32) + output_terms).astype(jnp.bfloat16)
    return decoded.reshape(text_rows, 1, D)


def solution(mesh):
    placed = (
        P("seq", None),
        P("seq", None),
        P("seq"),
        P(),
        P(None, "seq", None),
        P(),
        P(None, None, "section"),
        P("section", None),
        P("section", None, None),
        P(None, "section"),
        P(None, None, "section"),
        P("section", None),
    )
    return jax.shard_map(
        body, mesh=mesh, in_specs=placed, out_specs=P(None, "seq", None), check_vma=False
    )
```

```python
import math

import jax
import jax.numpy as jnp
from jax import lax
from jax.sharding import PartitionSpec as P
from jax.experimental import pallas as pl
from jax.experimental.pallas import tpu as pltpu
import functools

D = 1408
HEAD = 88


def layer_norm(values):
    values = values.astype(jnp.float32)
    centred = values - jnp.mean(values, -1, keepdims=True)
    return centred * lax.rsqrt(jnp.mean(centred * centred, -1, keepdims=True) + 1e-06)


def root_norm(values):
    values = values.astype(jnp.float32)
    return values * lax.rsqrt(jnp.mean(values * values, -1, keepdims=True) + 1e-06)


def merge_rows(grid, offsets, count):
    heights = grid[:, 0]
    widths = grid[:, 1]
    group_start = offsets // 4
    group_count = heights * widths // 4
    merged_ids = jnp.arange(count, dtype=jnp.int32)
    inside = (
        (merged_ids[:, None] >= group_start[None, :])
        & (merged_ids[:, None] < (group_start + group_count)[None, :])
    ).astype(jnp.int32)
    first_group = jnp.sum(inside * group_start[None, :], 1)
    first_patch = jnp.sum(inside * offsets[None, :], 1)
    row_width = jnp.sum(inside * widths[None, :], 1)
    within = merged_ids - first_group
    groups_across = row_width // 2
    group_row = within // groups_across
    group_col = within % groups_across
    corner = first_patch + 2 * group_row * row_width + 2 * group_col
    return jnp.stack([corner, corner + 1, corner + row_width, corner + row_width + 1], 1)


def _text_kernel(q_ref, kv_ref, qpos_ref, qseg_ref, kpos_ref, kseg_ref, o_ref, acc_ref, tot_ref, *, scale):
    qb = pl.program_id(0)
    kb = pl.program_id(1)
    heads, rows, head = q_ref.shape

    @pl.when(kb == 0)
    def _():
        acc_ref[...] = jnp.zeros_like(acc_ref)
        tot_ref[...] = jnp.zeros_like(tot_ref)

    @pl.when(kb <= qb)
    def _():
        q = q_ref[...].reshape(heads * rows, head)
        shards, _, krows, _ = kv_ref.shape
        k = kv_ref[:, 0].reshape(shards * krows, head)
        v = kv_ref[:, 1].reshape(shards * krows, head)
        s = lax.dot_general(q, k, (((1,), (1,)), ((), ())), preferred_element_type=jnp.float32) * scale
        allowed = (kpos_ref[0] <= qpos_ref[0]) & (kseg_ref[0] == qseg_ref[0])
        w = jnp.where(allowed, jnp.exp(s), 0.0)
        tot_ref[...] += jnp.sum(w, -1, keepdims=True)
        acc_ref[...] += jnp.dot(w.astype(jnp.bfloat16), v, preferred_element_type=jnp.float32)

    @pl.when(kb == pl.num_programs(1) - 1)
    def _():
        o_ref[...] = (acc_ref[...] / tot_ref[...]).astype(o_ref.dtype).reshape(o_ref.shape)


def text_attention(q, kv, qpos, qseg, kpos, kseg, rows, scale):
    heads, text_rows, head = q.shape
    shards = kv.shape[0]
    blocks = text_rows // rows
    return pl.pallas_call(
        functools.partial(_text_kernel, scale=scale),
        grid=(blocks, blocks),
        in_specs=[
            pl.BlockSpec((heads, rows, head), lambda i, j: (0, i, 0)),
            pl.BlockSpec((shards, 2, rows, head), lambda i, j: (0, 0, jnp.minimum(i, j), 0)),
            pl.BlockSpec((1, heads * rows, 1), lambda i, j: (i, 0, 0)),
            pl.BlockSpec((1, heads * rows, 1), lambda i, j: (i, 0, 0)),
            pl.BlockSpec((1, 1, shards * rows), lambda i, j: (jnp.minimum(i, j), 0, 0)),
            pl.BlockSpec((1, 1, shards * rows), lambda i, j: (jnp.minimum(i, j), 0, 0)),
        ],
        out_specs=pl.BlockSpec((heads, rows, head), lambda i, j: (0, i, 0)),
        out_shape=jax.ShapeDtypeStruct((heads, text_rows, head), jnp.bfloat16),
        scratch_shapes=[pltpu.VMEM((heads * rows, head), jnp.float32), pltpu.VMEM((heads * rows, 1), jnp.float32)],
        compiler_params=pltpu.CompilerParams(dimension_semantics=("arbitrary", "arbitrary")),
    )(q, kv, qpos, qseg, kpos, kseg)


def swap(values):
    return lax.ppermute(values, "section", [(0, 1), (1, 0)])


def in_head_order(first, own, other, axis):
    return jnp.where(
        first, jnp.concatenate([own, other], axis), jnp.concatenate([other, own], axis)
    )


def body(
    patches,
    image_grid,
    image_offsets,
    dest_positions,
    text_embeds,
    segment_ids,
    vision_qkv,
    vision_out,
    projector,
    decoder_q,
    decoder_kv,
    decoder_out,
):
    section_index = lax.axis_index("section")
    seq_index = lax.axis_index("seq")
    seq_count = lax.axis_size("seq")
    first = section_index == 0
    scale = 3.0 / math.sqrt(HEAD)
    patch_count = patches.shape[0]
    local_heads = vision_out.shape[0] // HEAD
    merged_count = patch_count // 4

    vision_out_other = swap(vision_out)
    decoder_out_full = in_head_order(first, decoder_out, swap(decoder_out), 0)

    normed = layer_norm(patches).astype(jnp.bfloat16)
    mixed = jnp.dot(normed, vision_qkv.reshape(D, -1), preferred_element_type=jnp.float32).reshape(
        patch_count, 3, local_heads, HEAD
    )
    queries = root_norm(mixed[:, 0]).astype(jnp.bfloat16)
    keys = root_norm(mixed[:, 1]).astype(jnp.bfloat16)
    values = mixed[:, 2].astype(jnp.bfloat16)
    offsets = image_offsets - seq_index * patch_count
    image_of = jnp.sum(
        (jnp.arange(patch_count, dtype=jnp.int32)[:, None] >= offsets[None, :]).astype(jnp.int32), 1
    )
    scores = jnp.einsum("qhd,khd->hqk", queries, keys, preferred_element_type=jnp.float32) * scale
    same = (image_of[:, None] == image_of[None, :])[None]
    weights = jnp.where(same, jnp.exp(scores), jnp.zeros_like(scores))
    totals = jnp.sum(weights, -1)
    mixed_values = jnp.einsum(
        "hqk,khd->qhd", weights.astype(jnp.bfloat16), values, preferred_element_type=jnp.float32
    )
    attended = (
        (mixed_values / jnp.transpose(totals)[:, :, None])
        .astype(jnp.bfloat16)
        .reshape(patch_count, local_heads * HEAD)
    )
    picks = merge_rows(image_grid, offsets, merged_count)
    own_picks = lax.dynamic_slice_in_dim(picks, 2 * section_index, 2, 1).reshape(-1)
    other_picks = lax.dynamic_slice_in_dim(picks, 2 - 2 * section_index, 2, 1).reshape(-1)
    received_heads = swap(attended[other_picks])
    own_rows = jnp.concatenate([attended[own_picks], received_heads], 1)
    full_out = jnp.concatenate([vision_out, vision_out_other], 0)
    kept = (
        patches[own_picks].astype(jnp.float32)
        + jnp.dot(own_rows, full_out, preferred_element_type=jnp.float32)
    ).astype(jnp.bfloat16)
    merge_terms = jnp.dot(
        kept.reshape(merged_count, 2 * D),
        projector.reshape(2 * D, D),
        preferred_element_type=jnp.float32,
    )
    image_rows = (merge_terms + swap(merge_terms)).astype(jnp.bfloat16)

    per_peer = merged_count // seq_count
    run_starts = dest_positions.reshape(seq_count, merged_count)[:, 0]
    own_start = run_starts[seq_index]
    received = lax.all_to_all(
        jnp.roll(image_rows.reshape(per_peer, seq_count, image_rows.shape[1]), own_start, axis=1),
        "seq",
        split_axis=1,
        concat_axis=1,
        tiled=True,
    )
    slot_base = jnp.arange(per_peer, dtype=jnp.int32)[:, None] * seq_count
    landing = (
        run_starts[None, :] + slot_base + (seq_index - run_starts[None, :]) % seq_count
    ) // seq_count
    text_rows = text_embeds.shape[0]
    prompt = text_embeds.reshape(text_rows, D).at[landing.reshape(-1)].set(received.reshape(-1, D))
    text_normed = root_norm(prompt).astype(jnp.bfloat16)
    text_queries = root_norm(
        jnp.dot(text_normed, decoder_q, preferred_element_type=jnp.float32).reshape(
            text_rows, local_heads, HEAD
        )
    ).astype(jnp.bfloat16)
    paired = jnp.dot(
        text_normed, decoder_kv.reshape(D, -1), preferred_element_type=jnp.float32
    ).reshape(text_rows, 2, HEAD)
    key_rows = root_norm(paired[:, 0]).astype(jnp.bfloat16)
    value_rows = paired[:, 1].astype(jnp.bfloat16)

    shared = jnp.stack([key_rows, value_rows], 0)[None]
    piece = lax.all_gather(shared, "seq", axis=0, tiled=True)
    rows = 32
    blocks = text_rows // rows
    query_places = jnp.arange(text_rows, dtype=jnp.int32) * seq_count + seq_index
    query_segments = lax.dynamic_slice_in_dim(segment_ids, seq_index, 1, 1)[:, 0]

    def per_query_row(values):
        spread = jnp.broadcast_to(values.reshape(blocks, 1, rows), (blocks, local_heads, rows))
        return spread.reshape(blocks, local_heads * rows, 1)

    def per_key(values):
        return jnp.transpose(values.reshape(seq_count, blocks, rows), (1, 0, 2)).reshape(
            blocks, 1, seq_count * rows
        )

    key_places = (
        jnp.arange(text_rows, dtype=jnp.int32)[None, :] * seq_count
        + jnp.arange(seq_count, dtype=jnp.int32)[:, None]
    )
    head_major = text_attention(
        jnp.transpose(text_queries, (1, 0, 2)),
        piece,
        per_query_row(query_places),
        per_query_row(query_segments),
        per_key(key_places),
        per_key(jnp.transpose(segment_ids)),
        rows,
        scale,
    )
    attended_text = jnp.transpose(head_major, (1, 0, 2)).reshape(text_rows, -1)
    all_heads = in_head_order(first, attended_text, swap(attended_text), 1)
    output_terms = jnp.dot(all_heads, decoder_out_full, preferred_element_type=jnp.float32)
    decoded = (prompt.astype(jnp.float32) + output_terms).astype(jnp.bfloat16)
    return decoded.reshape(text_rows, 1, D)


def solution(mesh):
    placed = (
        P("seq", None),
        P("seq", None),
        P("seq"),
        P(),
        P(None, "seq", None),
        P(),
        P(None, None, "section"),
        P("section", None),
        P("section", None, None),
        P(None, "section"),
        P(None, None, "section"),
        P("section", None),
    )
    return jax.shard_map(
        body, mesh=mesh, in_specs=placed, out_specs=P(None, "seq", None), check_vma=False
    )
```

```python
import math

import jax
import jax.numpy as jnp
from jax import lax
from jax.sharding import PartitionSpec as P
from jax.experimental import pallas as pl
from jax.experimental.pallas import tpu as pltpu
import functools

D = 1408
HEAD = 88


def layer_norm(values):
    values = values.astype(jnp.float32)
    centred = values - jnp.mean(values, -1, keepdims=True)
    return centred * lax.rsqrt(jnp.mean(centred * centred, -1, keepdims=True) + 1e-06)


def root_norm(values):
    values = values.astype(jnp.float32)
    return values * lax.rsqrt(jnp.mean(values * values, -1, keepdims=True) + 1e-06)


def merge_rows(grid, offsets, count):
    heights = grid[:, 0]
    widths = grid[:, 1]
    group_start = offsets // 4
    group_count = heights * widths // 4
    merged_ids = jnp.arange(count, dtype=jnp.int32)
    inside = (
        (merged_ids[:, None] >= group_start[None, :])
        & (merged_ids[:, None] < (group_start + group_count)[None, :])
    ).astype(jnp.int32)
    first_group = jnp.sum(inside * group_start[None, :], 1)
    first_patch = jnp.sum(inside * offsets[None, :], 1)
    row_width = jnp.sum(inside * widths[None, :], 1)
    within = merged_ids - first_group
    groups_across = row_width // 2
    group_row = within // groups_across
    group_col = within % groups_across
    corner = first_patch + 2 * group_row * row_width + 2 * group_col
    return jnp.stack([corner, corner + 1, corner + row_width, corner + row_width + 1], 1)


def _segment_start(info_ref, places):
    start = jnp.zeros_like(places) + info_ref[0]
    for doc in range(1, 4):
        bound = info_ref[doc]
        start = jnp.where(places >= bound, bound, start)
    return start


def _text_kernel(info_ref, q_ref, kv_ref, o_ref, acc_ref, tot_ref, *, scale):
    qb = pl.program_id(0)
    kb = pl.program_id(1)
    heads, rows, head = q_ref.shape
    shards = kv_ref.shape[0]
    span = rows * shards
    own = info_ref[4]
    first_query = qb * span + own
    last_query = first_query + (rows - 1) * shards
    first_block = _segment_start(info_ref, first_query) // span
    active = (kb >= first_block) & (kb <= qb)
    unmasked = (kb < qb) & (kb * span >= _segment_start(info_ref, last_query))

    @pl.when(kb == 0)
    def _():
        acc_ref[...] = jnp.zeros_like(acc_ref)
        tot_ref[...] = jnp.zeros_like(tot_ref)

    def accumulate(masked):
        q = q_ref[...].reshape(heads * rows, head)
        k = kv_ref[:, 0].reshape(span, head)
        v = kv_ref[:, 1].reshape(span, head)
        s = lax.dot_general(q, k, (((1,), (1,)), ((), ())), preferred_element_type=jnp.float32)
        w = jnp.exp(s * scale)
        if masked:
            row = lax.broadcasted_iota(jnp.int32, (heads * rows, 1), 0) & (rows - 1)
            query_places = (qb * rows + row) * shards + own
            lane = lax.broadcasted_iota(jnp.int32, (1, span), 1)
            key_places = (kb * rows + (lane & (rows - 1))) * shards + lax.shift_right_logical(
                lane, rows.bit_length() - 1
            )
            allowed = (key_places <= query_places) & (
                key_places >= _segment_start(info_ref, query_places)
            )
            w = jnp.where(allowed, w, 0.0)
        tot_ref[...] += jnp.sum(w, -1, keepdims=True)
        acc_ref[...] += jnp.dot(w.astype(jnp.bfloat16), v, preferred_element_type=jnp.float32)

    @pl.when(active & unmasked)
    def _():
        accumulate(False)

    @pl.when(active & jnp.logical_not(unmasked))
    def _():
        accumulate(True)

    @pl.when(kb == pl.num_programs(1) - 1)
    def _():
        o_ref[...] = (acc_ref[...] / tot_ref[...]).astype(o_ref.dtype).reshape(o_ref.shape)


def text_attention(info, q, kv, rows, scale):
    heads, text_rows, head = q.shape
    shards = kv.shape[0]
    blocks = text_rows // rows
    span = rows * shards

    def kv_block(i, j, info_ref):
        first_block = _segment_start(info_ref, i * span + info_ref[4]) // span
        return (0, 0, jnp.maximum(jnp.minimum(i, j), first_block), 0)

    return pl.pallas_call(
        functools.partial(_text_kernel, scale=scale),
        grid_spec=pltpu.PrefetchScalarGridSpec(
            num_scalar_prefetch=1,
            grid=(blocks, blocks),
            in_specs=[
                pl.BlockSpec((heads, rows, head), lambda i, j, info_ref: (0, i, 0)),
                pl.BlockSpec((shards, 2, rows, head), kv_block),
            ],
            out_specs=pl.BlockSpec((heads, rows, head), lambda i, j, info_ref: (0, i, 0)),
            scratch_shapes=[
                pltpu.VMEM((heads * rows, head), jnp.float32),
                pltpu.VMEM((heads * rows, 1), jnp.float32),
            ],
        ),
        out_shape=jax.ShapeDtypeStruct((heads, text_rows, head), jnp.bfloat16),
        compiler_params=pltpu.CompilerParams(dimension_semantics=("arbitrary", "arbitrary")),
    )(info, q, kv)


def swap(values):
    return lax.ppermute(values, "section", [(0, 1), (1, 0)])


def in_head_order(first, own, other, axis):
    return jnp.where(
        first, jnp.concatenate([own, other], axis), jnp.concatenate([other, own], axis)
    )


def body(
    patches,
    image_grid,
    image_offsets,
    dest_positions,
    text_embeds,
    segment_ids,
    vision_qkv,
    vision_out,
    projector,
    decoder_q,
    decoder_kv,
    decoder_out,
):
    section_index = lax.axis_index("section")
    seq_index = lax.axis_index("seq")
    seq_count = lax.axis_size("seq")
    first = section_index == 0
    scale = 3.0 / math.sqrt(HEAD)
    patch_count = patches.shape[0]
    local_heads = vision_out.shape[0] // HEAD
    merged_count = patch_count // 4

    vision_out_other = swap(vision_out)
    decoder_out_full = in_head_order(first, decoder_out, swap(decoder_out), 0)

    normed = layer_norm(patches).astype(jnp.bfloat16)
    mixed = jnp.dot(normed, vision_qkv.reshape(D, -1), preferred_element_type=jnp.float32).reshape(
        patch_count, 3, local_heads, HEAD
    )
    queries = root_norm(mixed[:, 0]).astype(jnp.bfloat16)
    keys = root_norm(mixed[:, 1]).astype(jnp.bfloat16)
    values = mixed[:, 2].astype(jnp.bfloat16)
    offsets = image_offsets - seq_index * patch_count
    image_of = jnp.sum(
        (jnp.arange(patch_count, dtype=jnp.int32)[:, None] >= offsets[None, :]).astype(jnp.int32), 1
    )
    scores = jnp.einsum("qhd,khd->hqk", queries, keys, preferred_element_type=jnp.float32) * scale
    same = (image_of[:, None] == image_of[None, :])[None]
    weights = jnp.where(same, jnp.exp(scores), jnp.zeros_like(scores))
    totals = jnp.sum(weights, -1)
    mixed_values = jnp.einsum(
        "hqk,khd->qhd", weights.astype(jnp.bfloat16), values, preferred_element_type=jnp.float32
    )
    attended = (
        (mixed_values / jnp.transpose(totals)[:, :, None])
        .astype(jnp.bfloat16)
        .reshape(patch_count, local_heads * HEAD)
    )
    picks = merge_rows(image_grid, offsets, merged_count)
    own_picks = lax.dynamic_slice_in_dim(picks, 2 * section_index, 2, 1).reshape(-1)
    other_picks = lax.dynamic_slice_in_dim(picks, 2 - 2 * section_index, 2, 1).reshape(-1)
    received_heads = swap(attended[other_picks])
    own_rows = jnp.concatenate([attended[own_picks], received_heads], 1)
    full_out = jnp.concatenate([vision_out, vision_out_other], 0)
    kept = (
        patches[own_picks].astype(jnp.float32)
        + jnp.dot(own_rows, full_out, preferred_element_type=jnp.float32)
    ).astype(jnp.bfloat16)
    merge_terms = jnp.dot(
        kept.reshape(merged_count, 2 * D),
        projector.reshape(2 * D, D),
        preferred_element_type=jnp.float32,
    )
    image_rows = (merge_terms + swap(merge_terms)).astype(jnp.bfloat16)

    per_peer = merged_count // seq_count
    run_starts = dest_positions.reshape(seq_count, merged_count)[:, 0]
    own_start = run_starts[seq_index]
    received = lax.all_to_all(
        jnp.roll(image_rows.reshape(per_peer, seq_count, image_rows.shape[1]), own_start, axis=1),
        "seq",
        split_axis=1,
        concat_axis=1,
        tiled=True,
    )
    slot_base = jnp.arange(per_peer, dtype=jnp.int32)[:, None] * seq_count
    landing = (
        run_starts[None, :] + slot_base + (seq_index - run_starts[None, :]) % seq_count
    ) // seq_count
    text_rows = text_embeds.shape[0]
    prompt = text_embeds.reshape(text_rows, D).at[landing.reshape(-1)].set(received.reshape(-1, D))
    text_normed = root_norm(prompt).astype(jnp.bfloat16)
    text_queries = root_norm(
        jnp.dot(text_normed, decoder_q, preferred_element_type=jnp.float32).reshape(
            text_rows, local_heads, HEAD
        )
    ).astype(jnp.bfloat16)
    paired = jnp.dot(
        text_normed, decoder_kv.reshape(D, -1), preferred_element_type=jnp.float32
    ).reshape(text_rows, 2, HEAD)
    key_rows = root_norm(paired[:, 0]).astype(jnp.bfloat16)
    value_rows = paired[:, 1].astype(jnp.bfloat16)

    shared = jnp.stack([key_rows, value_rows], 0)[None]
    piece = lax.all_gather(shared, "seq", axis=0, tiled=True)
    rows = 32
    doc_starts = jnp.sum(
        (segment_ids[None] < jnp.arange(4, dtype=jnp.int32)[:, None, None]).astype(jnp.int32),
        (1, 2),
    )
    info = jnp.concatenate(
        [doc_starts, jnp.full((1,), seq_index, jnp.int32), jnp.zeros((3,), jnp.int32)]
    )
    head_major = text_attention(info, jnp.transpose(text_queries, (1, 0, 2)), piece, rows, scale)
    attended_text = jnp.transpose(head_major, (1, 0, 2)).reshape(text_rows, -1)
    all_heads = in_head_order(first, attended_text, swap(attended_text), 1)
    output_terms = jnp.dot(all_heads, decoder_out_full, preferred_element_type=jnp.float32)
    decoded = (prompt.astype(jnp.float32) + output_terms).astype(jnp.bfloat16)
    return decoded.reshape(text_rows, 1, D)


def solution(mesh):
    placed = (
        P("seq", None),
        P("seq", None),
        P("seq"),
        P(),
        P(None, "seq", None),
        P(),
        P(None, None, "section"),
        P("section", None),
        P("section", None, None),
        P(None, "section"),
        P(None, None, "section"),
        P("section", None),
    )
    return jax.shard_map(
        body, mesh=mesh, in_specs=placed, out_specs=P(None, "seq", None), check_vma=False
    )
```

```python
import math

import jax
import jax.numpy as jnp
from jax import lax
from jax.sharding import PartitionSpec as P
from jax.experimental import pallas as pl
from jax.experimental.pallas import tpu as pltpu
import functools

D = 1408
HEAD = 88


def layer_norm(values):
    values = values.astype(jnp.float32)
    centred = values - jnp.mean(values, -1, keepdims=True)
    return centred * lax.rsqrt(jnp.mean(centred * centred, -1, keepdims=True) + 1e-06)


def root_norm(values):
    values = values.astype(jnp.float32)
    return values * lax.rsqrt(jnp.mean(values * values, -1, keepdims=True) + 1e-06)


def merge_rows(grid, offsets, count):
    heights = grid[:, 0]
    widths = grid[:, 1]
    group_start = offsets // 4
    group_count = heights * widths // 4
    merged_ids = jnp.arange(count, dtype=jnp.int32)
    inside = (
        (merged_ids[:, None] >= group_start[None, :])
        & (merged_ids[:, None] < (group_start + group_count)[None, :])
    ).astype(jnp.int32)
    first_group = jnp.sum(inside * group_start[None, :], 1)
    first_patch = jnp.sum(inside * offsets[None, :], 1)
    row_width = jnp.sum(inside * widths[None, :], 1)
    within = merged_ids - first_group
    groups_across = row_width // 2
    group_row = within // groups_across
    group_col = within % groups_across
    corner = first_patch + 2 * group_row * row_width + 2 * group_col
    return jnp.stack([corner, corner + 1, corner + row_width, corner + row_width + 1], 1)


def _segment_start(info_ref, places):
    start = jnp.zeros_like(places) + info_ref[0]
    for doc in range(1, 4):
        bound = info_ref[doc]
        start = jnp.where(places >= bound, bound, start)
    return start


def _text_kernel(info_ref, q_ref, kv_ref, o_ref, acc_ref, tot_ref, *, scale):
    qb = pl.program_id(0)
    kb = pl.program_id(1)
    heads, rows, head = q_ref.shape
    shards = kv_ref.shape[0]
    span = rows * shards
    own = info_ref[4]
    first_query = qb * span + own
    last_query = first_query + (rows - 1) * shards
    first_block = _segment_start(info_ref, first_query) // span
    active = (kb >= first_block) & (kb <= qb)
    unmasked = (kb < qb) & (kb * span >= _segment_start(info_ref, last_query))

    @pl.when(kb == 0)
    def _():
        acc_ref[...] = jnp.zeros_like(acc_ref)
        tot_ref[...] = jnp.zeros_like(tot_ref)

    def accumulate(masked):
        q = q_ref[...].reshape(heads * rows, head)
        k = kv_ref[:, 0].reshape(span, head)
        v = kv_ref[:, 1].reshape(span, head)
        s = lax.dot_general(q, k, (((1,), (1,)), ((), ())), preferred_element_type=jnp.float32)
        w = jnp.exp(s * scale)
        if masked:
            row = lax.broadcasted_iota(jnp.int32, (heads * rows, 1), 0) & (rows - 1)
            query_places = (qb * rows + row) * shards + own
            lane = lax.broadcasted_iota(jnp.int32, (1, span), 1)
            key_places = (kb * rows + (lane & (rows - 1))) * shards + lax.shift_right_logical(
                lane, rows.bit_length() - 1
            )
            allowed = (key_places <= query_places) & (
                key_places >= _segment_start(info_ref, query_places)
            )
            w = jnp.where(allowed, w, 0.0)
        tot_ref[...] += jnp.sum(w, -1, keepdims=True)
        acc_ref[...] += jnp.dot(w.astype(jnp.bfloat16), v, preferred_element_type=jnp.float32)

    @pl.when(active & unmasked)
    def _():
        accumulate(False)

    @pl.when(active & jnp.logical_not(unmasked))
    def _():
        accumulate(True)

    @pl.when(kb == pl.num_programs(1) - 1)
    def _():
        o_ref[...] = (acc_ref[...] / tot_ref[...]).astype(o_ref.dtype).reshape(o_ref.shape)


def text_attention(info, q, kv, rows, scale):
    heads, text_rows, head = q.shape
    shards = kv.shape[0]
    blocks = text_rows // rows
    span = rows * shards

    def kv_block(i, j, info_ref):
        first_block = _segment_start(info_ref, i * span + info_ref[4]) // span
        return (0, 0, jnp.maximum(jnp.minimum(i, j), first_block), 0)

    return pl.pallas_call(
        functools.partial(_text_kernel, scale=scale),
        grid_spec=pltpu.PrefetchScalarGridSpec(
            num_scalar_prefetch=1,
            grid=(blocks, blocks),
            in_specs=[
                pl.BlockSpec((heads, rows, head), lambda i, j, info_ref: (0, i, 0)),
                pl.BlockSpec((shards, 2, rows, head), kv_block),
            ],
            out_specs=pl.BlockSpec((heads, rows, head), lambda i, j, info_ref: (0, i, 0)),
            scratch_shapes=[
                pltpu.VMEM((heads * rows, head), jnp.float32),
                pltpu.VMEM((heads * rows, 1), jnp.float32),
            ],
        ),
        out_shape=jax.ShapeDtypeStruct((heads, text_rows, head), jnp.bfloat16),
        compiler_params=pltpu.CompilerParams(dimension_semantics=("arbitrary", "arbitrary")),
    )(info, q, kv)


def swap(values):
    return lax.ppermute(values, "section", [(0, 1), (1, 0)])


def in_head_order(first, own, other, axis):
    return jnp.where(
        first, jnp.concatenate([own, other], axis), jnp.concatenate([other, own], axis)
    )


def body(
    patches,
    image_grid,
    image_offsets,
    dest_positions,
    text_embeds,
    segment_ids,
    vision_qkv,
    vision_out,
    projector,
    decoder_q,
    decoder_kv,
    decoder_out,
):
    section_index = lax.axis_index("section")
    seq_index = lax.axis_index("seq")
    seq_count = lax.axis_size("seq")
    first = section_index == 0
    scale = 3.0 / math.sqrt(HEAD)
    patch_count = patches.shape[0]
    local_heads = vision_out.shape[0] // HEAD
    merged_count = patch_count // 4

    vision_out_other = swap(vision_out)
    decoder_out_full = in_head_order(first, decoder_out, swap(decoder_out), 0)

    normed = layer_norm(patches).astype(jnp.bfloat16)
    mixed = jnp.dot(normed, vision_qkv.reshape(D, -1), preferred_element_type=jnp.float32).reshape(
        patch_count, 3, local_heads, HEAD
    )
    queries = root_norm(mixed[:, 0]).astype(jnp.bfloat16)
    keys = root_norm(mixed[:, 1]).astype(jnp.bfloat16)
    values = mixed[:, 2].astype(jnp.bfloat16)
    offsets = image_offsets - seq_index * patch_count
    image_of = jnp.sum(
        (jnp.arange(patch_count, dtype=jnp.int32)[:, None] >= offsets[None, :]).astype(jnp.int32), 1
    )
    scores = jnp.einsum("qhd,khd->hqk", queries, keys, preferred_element_type=jnp.float32) * scale
    same = (image_of[:, None] == image_of[None, :])[None]
    weights = jnp.where(same, jnp.exp(scores), jnp.zeros_like(scores))
    totals = jnp.sum(weights, -1)
    mixed_values = jnp.einsum(
        "hqk,khd->qhd", weights.astype(jnp.bfloat16), values, preferred_element_type=jnp.float32
    )
    attended = (
        (mixed_values / jnp.transpose(totals)[:, :, None])
        .astype(jnp.bfloat16)
        .reshape(patch_count, local_heads * HEAD)
    )
    picks = merge_rows(image_grid, offsets, merged_count)
    own_picks = lax.dynamic_slice_in_dim(picks, 2 * section_index, 2, 1).reshape(-1)
    other_picks = lax.dynamic_slice_in_dim(picks, 2 - 2 * section_index, 2, 1).reshape(-1)
    patch_ids = jnp.arange(patch_count, dtype=jnp.int32)[None, :]
    own_select = (own_picks[:, None] == patch_ids).astype(jnp.bfloat16)
    other_select = (other_picks[:, None] == patch_ids).astype(jnp.bfloat16)
    received_heads = swap(
        jnp.dot(other_select, attended, preferred_element_type=jnp.float32).astype(jnp.bfloat16)
    )
    own_heads = jnp.dot(own_select, attended, preferred_element_type=jnp.float32).astype(
        jnp.bfloat16
    )
    own_rows = jnp.concatenate([own_heads, received_heads], 1)
    full_out = jnp.concatenate([vision_out, vision_out_other], 0)
    kept = (
        jnp.dot(own_select, patches, preferred_element_type=jnp.float32)
        + jnp.dot(own_rows, full_out, preferred_element_type=jnp.float32)
    ).astype(jnp.bfloat16)
    merge_terms = jnp.dot(
        kept.reshape(merged_count, 2 * D),
        projector.reshape(2 * D, D),
        preferred_element_type=jnp.float32,
    )
    image_rows = (merge_terms + swap(merge_terms)).astype(jnp.bfloat16)

    per_peer = merged_count // seq_count
    run_starts = dest_positions.reshape(seq_count, merged_count)[:, 0]
    own_start = run_starts[seq_index]
    received = lax.all_to_all(
        jnp.roll(image_rows.reshape(per_peer, seq_count, image_rows.shape[1]), own_start, axis=1),
        "seq",
        split_axis=1,
        concat_axis=1,
        tiled=True,
    )
    slot_base = jnp.arange(per_peer, dtype=jnp.int32)[:, None] * seq_count
    landing = (
        run_starts[None, :] + slot_base + (seq_index - run_starts[None, :]) % seq_count
    ) // seq_count
    text_rows = text_embeds.shape[0]
    prompt = text_embeds.reshape(text_rows, D).at[landing.reshape(-1)].set(received.reshape(-1, D))
    text_normed = root_norm(prompt).astype(jnp.bfloat16)
    head_queries = root_norm(
        jnp.einsum(
            "td,dhe->hte",
            text_normed,
            decoder_q.reshape(D, local_heads, HEAD),
            preferred_element_type=jnp.float32,
        )
    ).astype(jnp.bfloat16)
    paired = jnp.dot(
        text_normed, decoder_kv.reshape(D, -1), preferred_element_type=jnp.float32
    ).reshape(text_rows, 2, HEAD)
    key_rows = root_norm(paired[:, 0]).astype(jnp.bfloat16)
    value_rows = paired[:, 1].astype(jnp.bfloat16)

    shared = jnp.stack([key_rows, value_rows], 0)[None]
    piece = lax.all_gather(shared, "seq", axis=0, tiled=True)
    rows = 32
    doc_starts = jnp.sum(
        (segment_ids[None] < jnp.arange(4, dtype=jnp.int32)[:, None, None]).astype(jnp.int32),
        (1, 2),
    )
    info = jnp.concatenate(
        [doc_starts, jnp.full((1,), seq_index, jnp.int32), jnp.zeros((3,), jnp.int32)]
    )
    head_major = text_attention(info, head_queries, piece, rows, scale)
    attended_text = jnp.transpose(head_major, (1, 0, 2)).reshape(text_rows, -1)
    all_heads = in_head_order(first, attended_text, swap(attended_text), 1)
    output_terms = jnp.dot(all_heads, decoder_out_full, preferred_element_type=jnp.float32)
    decoded = (prompt.astype(jnp.float32) + output_terms).astype(jnp.bfloat16)
    return decoded.reshape(text_rows, 1, D)


def solution(mesh):
    placed = (
        P("seq", None),
        P("seq", None),
        P("seq"),
        P(),
        P(None, "seq", None),
        P(),
        P(None, None, "section"),
        P("section", None),
        P("section", None, None),
        P(None, "section"),
        P(None, None, "section"),
        P("section", None),
    )
    return jax.shard_map(
        body, mesh=mesh, in_specs=placed, out_specs=P(None, "seq", None), check_vma=False
    )
```

```python
import math

import jax
import jax.numpy as jnp
from jax import lax
from jax.sharding import PartitionSpec as P
from jax.experimental import pallas as pl
from jax.experimental.pallas import tpu as pltpu
import functools

D = 1408
HEAD = 88


def layer_norm(values):
    values = values.astype(jnp.float32)
    centred = values - jnp.mean(values, -1, keepdims=True)
    return centred * lax.rsqrt(jnp.mean(centred * centred, -1, keepdims=True) + 1e-06)


def root_norm(values):
    values = values.astype(jnp.float32)
    return values * lax.rsqrt(jnp.mean(values * values, -1, keepdims=True) + 1e-06)


def merge_rows(grid, offsets, count):
    heights = grid[:, 0]
    widths = grid[:, 1]
    group_start = offsets // 4
    group_count = heights * widths // 4
    merged_ids = jnp.arange(count, dtype=jnp.int32)
    inside = (
        (merged_ids[:, None] >= group_start[None, :])
        & (merged_ids[:, None] < (group_start + group_count)[None, :])
    ).astype(jnp.int32)
    first_group = jnp.sum(inside * group_start[None, :], 1)
    first_patch = jnp.sum(inside * offsets[None, :], 1)
    row_width = jnp.sum(inside * widths[None, :], 1)
    within = merged_ids - first_group
    groups_across = row_width // 2
    group_row = within // groups_across
    group_col = within % groups_across
    corner = first_patch + 2 * group_row * row_width + 2 * group_col
    return jnp.stack([corner, corner + 1, corner + row_width, corner + row_width + 1], 1)


def _segment_start(info_ref, places):
    start = jnp.zeros_like(places) + info_ref[0]
    for doc in range(1, 4):
        bound = info_ref[doc]
        start = jnp.where(places >= bound, bound, start)
    return start


def _first_block(info_ref, qb, span):
    return _segment_start(info_ref, qb * span + info_ref[4]) // span


def _text_kernel(query_block_ref, key_block_ref, info_ref, q_ref, kv_ref, o_ref, acc_ref, tot_ref, *, scale):
    step = pl.program_id(0)
    qb = query_block_ref[step]
    kb = key_block_ref[step]
    heads, rows, head = q_ref.shape
    shards = kv_ref.shape[0]
    span = rows * shards
    own = info_ref[4]
    last_query = qb * span + own + (rows - 1) * shards
    active = kb >= _first_block(info_ref, qb, span)
    unmasked = (kb < qb) & (kb * span >= _segment_start(info_ref, last_query))

    @pl.when(kb == 0)
    def _():
        acc_ref[...] = jnp.zeros_like(acc_ref)
        tot_ref[...] = jnp.zeros_like(tot_ref)

    def accumulate(masked):
        q = q_ref[...].reshape(heads * rows, head)
        k = kv_ref[:, 0].reshape(span, head)
        v = kv_ref[:, 1].reshape(span, head)
        s = lax.dot_general(q, k, (((1,), (1,)), ((), ())), preferred_element_type=jnp.float32)
        w = jnp.exp(s * scale)
        if masked:
            row = lax.broadcasted_iota(jnp.int32, (heads * rows, 1), 0) & (rows - 1)
            query_places = (qb * rows + row) * shards + own
            lane = lax.broadcasted_iota(jnp.int32, (1, span), 1)
            key_places = (kb * rows + (lane & (rows - 1))) * shards + lax.shift_right_logical(
                lane, rows.bit_length() - 1
            )
            allowed = (key_places <= query_places) & (
                key_places >= _segment_start(info_ref, query_places)
            )
            w = jnp.where(allowed, w, 0.0)
        tot_ref[...] += jnp.sum(w, -1, keepdims=True)
        acc_ref[...] += jnp.dot(w.astype(jnp.bfloat16), v, preferred_element_type=jnp.float32)

    @pl.when(active & unmasked)
    def _():
        accumulate(False)

    @pl.when(active & jnp.logical_not(unmasked))
    def _():
        accumulate(True)

    @pl.when(kb == qb)
    def _():
        o_ref[...] = (acc_ref[...] / tot_ref[...]).astype(o_ref.dtype).reshape(o_ref.shape)


def text_attention(info, q, kv, rows, scale):
    heads, text_rows, head = q.shape
    shards = kv.shape[0]
    blocks = text_rows // rows
    span = rows * shards
    pairs = [(i, j) for i in range(blocks) for j in range(i + 1)]
    query_block = jnp.array([i for i, _ in pairs], jnp.int32)
    key_block = jnp.array([j for _, j in pairs], jnp.int32)

    def q_block(t, qb_ref, kb_ref, info_ref):
        return (0, qb_ref[t], 0)

    def kv_block(t, qb_ref, kb_ref, info_ref):
        qb = qb_ref[t]
        return (0, 0, jnp.maximum(kb_ref[t], _first_block(info_ref, qb, span)), 0)

    return pl.pallas_call(
        functools.partial(_text_kernel, scale=scale),
        grid_spec=pltpu.PrefetchScalarGridSpec(
            num_scalar_prefetch=3,
            grid=(len(pairs),),
            in_specs=[
                pl.BlockSpec((heads, rows, head), q_block),
                pl.BlockSpec((shards, 2, rows, head), kv_block),
            ],
            out_specs=pl.BlockSpec((heads, rows, head), q_block),
            scratch_shapes=[
                pltpu.VMEM((heads * rows, head), jnp.float32),
                pltpu.VMEM((heads * rows, 1), jnp.float32),
            ],
        ),
        out_shape=jax.ShapeDtypeStruct((heads, text_rows, head), jnp.bfloat16),
        compiler_params=pltpu.CompilerParams(dimension_semantics=("arbitrary",)),
    )(query_block, key_block, info, q, kv)


def swap(values):
    return lax.ppermute(values, "section", [(0, 1), (1, 0)])


def in_head_order(first, own, other, axis):
    return jnp.where(
        first, jnp.concatenate([own, other], axis), jnp.concatenate([other, own], axis)
    )


def body(
    patches,
    image_grid,
    image_offsets,
    dest_positions,
    text_embeds,
    segment_ids,
    vision_qkv,
    vision_out,
    projector,
    decoder_q,
    decoder_kv,
    decoder_out,
):
    section_index = lax.axis_index("section")
    seq_index = lax.axis_index("seq")
    seq_count = lax.axis_size("seq")
    first = section_index == 0
    scale = 3.0 / math.sqrt(HEAD)
    patch_count = patches.shape[0]
    local_heads = vision_out.shape[0] // HEAD
    merged_count = patch_count // 4

    vision_out_other = swap(vision_out)
    decoder_out_other = swap(decoder_out)

    normed = layer_norm(patches).astype(jnp.bfloat16)
    mixed = jnp.dot(normed, vision_qkv.reshape(D, -1), preferred_element_type=jnp.float32).reshape(
        patch_count, 3, local_heads, HEAD
    )
    queries = root_norm(mixed[:, 0]).astype(jnp.bfloat16)
    keys = root_norm(mixed[:, 1]).astype(jnp.bfloat16)
    values = mixed[:, 2].astype(jnp.bfloat16)
    offsets = image_offsets - seq_index * patch_count
    image_of = jnp.sum(
        (jnp.arange(patch_count, dtype=jnp.int32)[:, None] >= offsets[None, :]).astype(jnp.int32), 1
    )
    scores = jnp.einsum("qhd,khd->hqk", queries, keys, preferred_element_type=jnp.float32) * scale
    same = (image_of[:, None] == image_of[None, :])[None]
    weights = jnp.where(same, jnp.exp(scores), jnp.zeros_like(scores))
    totals = jnp.sum(weights, -1)
    mixed_values = jnp.einsum(
        "hqk,khd->qhd", weights.astype(jnp.bfloat16), values, preferred_element_type=jnp.float32
    )
    attended = (
        (mixed_values / jnp.transpose(totals)[:, :, None])
        .astype(jnp.bfloat16)
        .reshape(patch_count, local_heads * HEAD)
    )
    picks = merge_rows(image_grid, offsets, merged_count)
    own_picks = lax.dynamic_slice_in_dim(picks, 2 * section_index, 2, 1).reshape(-1)
    other_picks = lax.dynamic_slice_in_dim(picks, 2 - 2 * section_index, 2, 1).reshape(-1)
    patch_ids = jnp.arange(patch_count, dtype=jnp.int32)[None, :]
    own_select = (own_picks[:, None] == patch_ids).astype(jnp.bfloat16)
    other_select = (other_picks[:, None] == patch_ids).astype(jnp.bfloat16)
    received_heads = swap(
        jnp.dot(other_select, attended, preferred_element_type=jnp.float32).astype(jnp.bfloat16)
    )
    own_heads = jnp.dot(own_select, attended, preferred_element_type=jnp.float32).astype(
        jnp.bfloat16
    )
    decoder_out_full, received_heads = lax.optimization_barrier(
        (in_head_order(first, decoder_out, decoder_out_other, 0), received_heads)
    )
    own_rows = jnp.concatenate([own_heads, received_heads], 1)
    full_out = jnp.concatenate([vision_out, vision_out_other], 0)
    kept = (
        jnp.dot(own_select, patches, preferred_element_type=jnp.float32)
        + jnp.dot(own_rows, full_out, preferred_element_type=jnp.float32)
    ).astype(jnp.bfloat16)
    merge_terms = jnp.dot(
        kept.reshape(merged_count, 2 * D),
        projector.reshape(2 * D, D),
        preferred_element_type=jnp.float32,
    )
    image_rows = (merge_terms + swap(merge_terms)).astype(jnp.bfloat16)

    per_peer = merged_count // seq_count
    run_starts = dest_positions.reshape(seq_count, merged_count)[:, 0]
    own_start = run_starts[seq_index]
    received = lax.all_to_all(
        jnp.roll(image_rows.reshape(per_peer, seq_count, image_rows.shape[1]), own_start, axis=1),
        "seq",
        split_axis=1,
        concat_axis=1,
        tiled=True,
    )
    slot_base = jnp.arange(per_peer, dtype=jnp.int32)[:, None] * seq_count
    landing = (
        run_starts[None, :] + slot_base + (seq_index - run_starts[None, :]) % seq_count
    ) // seq_count
    text_rows = text_embeds.shape[0]
    prompt = text_embeds.reshape(text_rows, D).at[landing.reshape(-1)].set(received.reshape(-1, D))
    text_normed = root_norm(prompt).astype(jnp.bfloat16)
    head_queries = root_norm(
        jnp.einsum(
            "td,dhe->hte",
            text_normed,
            decoder_q.reshape(D, local_heads, HEAD),
            preferred_element_type=jnp.float32,
        )
    ).astype(jnp.bfloat16)
    paired = jnp.dot(
        text_normed, decoder_kv.reshape(D, -1), preferred_element_type=jnp.float32
    ).reshape(text_rows, 2, HEAD)
    key_rows = root_norm(paired[:, 0]).astype(jnp.bfloat16)
    value_rows = paired[:, 1].astype(jnp.bfloat16)

    shared = jnp.stack([key_rows, value_rows], 0)[None]
    piece = lax.all_gather(shared, "seq", axis=0, tiled=True)
    rows = 32
    doc_starts = jnp.sum(
        (segment_ids[None] < jnp.arange(4, dtype=jnp.int32)[:, None, None]).astype(jnp.int32),
        (1, 2),
    )
    info = jnp.concatenate(
        [doc_starts, jnp.full((1,), seq_index, jnp.int32), jnp.zeros((3,), jnp.int32)]
    )
    head_major = text_attention(info, head_queries, piece, rows, scale)
    attended_text = jnp.transpose(head_major, (1, 0, 2)).reshape(text_rows, -1)
    all_heads = in_head_order(first, attended_text, swap(attended_text), 1)
    output_terms = jnp.dot(all_heads, decoder_out_full, preferred_element_type=jnp.float32)
    decoded = (prompt.astype(jnp.float32) + output_terms).astype(jnp.bfloat16)
    return decoded.reshape(text_rows, 1, D)


def solution(mesh):
    placed = (
        P("seq", None),
        P("seq", None),
        P("seq"),
        P(),
        P(None, "seq", None),
        P(),
        P(None, None, "section"),
        P("section", None),
        P("section", None, None),
        P(None, "section"),
        P(None, None, "section"),
        P("section", None),
    )
    return jax.shard_map(
        body, mesh=mesh, in_specs=placed, out_specs=P(None, "seq", None), check_vma=False
    )
```

```python
import math

import jax
import jax.numpy as jnp
from jax import lax
from jax.sharding import PartitionSpec as P
from jax.experimental import pallas as pl
from jax.experimental.pallas import tpu as pltpu
import functools

D = 1408
HEAD = 88


def layer_norm(values):
    values = values.astype(jnp.float32)
    centred = values - jnp.mean(values, -1, keepdims=True)
    return centred * lax.rsqrt(jnp.mean(centred * centred, -1, keepdims=True) + 1e-06)


def root_norm(values):
    values = values.astype(jnp.float32)
    return values * lax.rsqrt(jnp.mean(values * values, -1, keepdims=True) + 1e-06)


def merge_rows(grid, offsets, count):
    heights = grid[:, 0]
    widths = grid[:, 1]
    group_start = offsets // 4
    group_count = heights * widths // 4
    merged_ids = jnp.arange(count, dtype=jnp.int32)
    inside = (
        (merged_ids[:, None] >= group_start[None, :])
        & (merged_ids[:, None] < (group_start + group_count)[None, :])
    ).astype(jnp.int32)
    first_group = jnp.sum(inside * group_start[None, :], 1)
    first_patch = jnp.sum(inside * offsets[None, :], 1)
    row_width = jnp.sum(inside * widths[None, :], 1)
    within = merged_ids - first_group
    groups_across = row_width // 2
    group_row = within // groups_across
    group_col = within % groups_across
    corner = first_patch + 2 * group_row * row_width + 2 * group_col
    return jnp.stack([corner, corner + 1, corner + row_width, corner + row_width + 1], 1)


def _segment_start(info_ref, places):
    start = jnp.zeros_like(places) + info_ref[0]
    for doc in range(1, 4):
        bound = info_ref[doc]
        start = jnp.where(places >= bound, bound, start)
    return start


def _first_block(info_ref, qb, span):
    return _segment_start(info_ref, qb * span + info_ref[4]) // span


def _text_kernel(query_block_ref, key_block_ref, info_ref, q_ref, kv_ref, o_ref, acc_ref, tot_ref, *, scale):
    step = pl.program_id(0)
    qb = query_block_ref[step]
    kb = key_block_ref[step]
    heads, rows, head = q_ref.shape
    shards = kv_ref.shape[0]
    span = rows * shards
    own = info_ref[4]
    last_query = qb * span + own + (rows - 1) * shards
    active = kb >= _first_block(info_ref, qb, span)
    unmasked = (kb < qb) & (kb * span >= _segment_start(info_ref, last_query))

    @pl.when(kb == 0)
    def _():
        acc_ref[...] = jnp.zeros_like(acc_ref)
        tot_ref[...] = jnp.zeros_like(tot_ref)

    def accumulate(masked):
        q = q_ref[...].reshape(heads * rows, head)
        k = kv_ref[:, 0].reshape(span, head)
        v = kv_ref[:, 1].reshape(span, head)
        s = lax.dot_general(q, k, (((1,), (1,)), ((), ())), preferred_element_type=jnp.float32)
        w = jnp.exp(s * scale)
        if masked:
            row = lax.broadcasted_iota(jnp.int32, (heads * rows, 1), 0) & (rows - 1)
            query_places = (qb * rows + row) * shards + own
            lane = lax.broadcasted_iota(jnp.int32, (1, span), 1)
            key_places = (kb * rows + (lane & (rows - 1))) * shards + lax.shift_right_logical(
                lane, rows.bit_length() - 1
            )
            allowed = (key_places <= query_places) & (
                key_places >= _segment_start(info_ref, query_places)
            )
            w = jnp.where(allowed, w, 0.0)
        tot_ref[...] += jnp.sum(w, -1, keepdims=True)
        acc_ref[...] += jnp.dot(w.astype(jnp.bfloat16), v, preferred_element_type=jnp.float32)

    @pl.when(active & unmasked)
    def _():
        accumulate(False)

    @pl.when(active & jnp.logical_not(unmasked))
    def _():
        accumulate(True)

    @pl.when(kb == qb)
    def _():
        o_ref[...] = (acc_ref[...] / tot_ref[...]).astype(o_ref.dtype).reshape(o_ref.shape)


def text_attention(info, q, kv, rows, scale):
    heads, text_rows, head = q.shape
    shards = kv.shape[0]
    blocks = text_rows // rows
    span = rows * shards
    pairs = [(i, j) for i in range(blocks) for j in range(i + 1)]
    query_block = jnp.array([i for i, _ in pairs], jnp.int32)
    key_block = jnp.array([j for _, j in pairs], jnp.int32)

    def q_block(t, qb_ref, kb_ref, info_ref):
        return (0, qb_ref[t], 0)

    def kv_block(t, qb_ref, kb_ref, info_ref):
        qb = qb_ref[t]
        return (0, 0, jnp.maximum(kb_ref[t], _first_block(info_ref, qb, span)), 0)

    return pl.pallas_call(
        functools.partial(_text_kernel, scale=scale),
        grid_spec=pltpu.PrefetchScalarGridSpec(
            num_scalar_prefetch=3,
            grid=(len(pairs),),
            in_specs=[
                pl.BlockSpec((heads, rows, head), q_block),
                pl.BlockSpec((shards, 2, rows, head), kv_block),
            ],
            out_specs=pl.BlockSpec((heads, rows, head), q_block),
            scratch_shapes=[
                pltpu.VMEM((heads * rows, head), jnp.float32),
                pltpu.VMEM((heads * rows, 1), jnp.float32),
            ],
        ),
        out_shape=jax.ShapeDtypeStruct((heads, text_rows, head), jnp.bfloat16),
        compiler_params=pltpu.CompilerParams(dimension_semantics=("arbitrary",)),
    )(query_block, key_block, info, q, kv)


def swap(values):
    return lax.ppermute(values, "section", [(0, 1), (1, 0)])


def in_head_order(first, own, other, axis):
    return jnp.where(
        first, jnp.concatenate([own, other], axis), jnp.concatenate([other, own], axis)
    )


def body(
    patches,
    image_grid,
    image_offsets,
    dest_positions,
    text_embeds,
    segment_ids,
    vision_qkv,
    vision_out,
    projector,
    decoder_q,
    decoder_kv,
    decoder_out,
):
    section_index = lax.axis_index("section")
    seq_index = lax.axis_index("seq")
    seq_count = lax.axis_size("seq")
    first = section_index == 0
    scale = 3.0 / math.sqrt(HEAD)
    patch_count = patches.shape[0]
    local_heads = vision_out.shape[0] // HEAD
    merged_count = patch_count // 4

    vision_out_other = swap(vision_out)
    decoder_out_other = swap(decoder_out)

    normed = layer_norm(patches).astype(jnp.bfloat16)
    mixed = jnp.dot(normed, vision_qkv.reshape(D, -1), preferred_element_type=jnp.float32).reshape(
        patch_count, 3, local_heads, HEAD
    )
    queries = root_norm(mixed[:, 0]).astype(jnp.bfloat16)
    keys = root_norm(mixed[:, 1]).astype(jnp.bfloat16)
    values = mixed[:, 2].astype(jnp.bfloat16)
    offsets = image_offsets - seq_index * patch_count
    image_of = jnp.sum(
        (jnp.arange(patch_count, dtype=jnp.int32)[:, None] >= offsets[None, :]).astype(jnp.int32), 1
    )
    scores = jnp.einsum("qhd,khd->hqk", queries, keys, preferred_element_type=jnp.float32) * scale
    same = (image_of[:, None] == image_of[None, :])[None]
    weights = jnp.where(same, jnp.exp(scores), jnp.zeros_like(scores))
    totals = jnp.sum(weights, -1)
    mixed_values = jnp.einsum(
        "hqk,khd->qhd", weights.astype(jnp.bfloat16), values, preferred_element_type=jnp.float32
    )
    attended = (
        (mixed_values / jnp.transpose(totals)[:, :, None])
        .astype(jnp.bfloat16)
        .reshape(patch_count, local_heads * HEAD)
    )
    picks = merge_rows(image_grid, offsets, merged_count)
    own_picks = lax.dynamic_slice_in_dim(picks, 2 * section_index, 2, 1).reshape(-1)
    other_picks = lax.dynamic_slice_in_dim(picks, 2 - 2 * section_index, 2, 1).reshape(-1)
    patch_ids = jnp.arange(patch_count, dtype=jnp.int32)[None, :]
    own_select = (own_picks[:, None] == patch_ids).astype(jnp.bfloat16)
    other_select = (other_picks[:, None] == patch_ids).astype(jnp.bfloat16)
    received_heads = swap(
        jnp.dot(other_select, attended, preferred_element_type=jnp.float32).astype(jnp.bfloat16)
    )
    own_heads = jnp.dot(own_select, attended, preferred_element_type=jnp.float32).astype(
        jnp.bfloat16
    )
    own_rows = jnp.concatenate([own_heads, received_heads], 1)
    full_out = jnp.concatenate([vision_out, vision_out_other], 0)
    kept = (
        jnp.dot(own_select, patches, preferred_element_type=jnp.float32)
        + jnp.dot(own_rows, full_out, preferred_element_type=jnp.float32)
    ).astype(jnp.bfloat16)
    merge_terms = jnp.dot(
        kept.reshape(merged_count, 2 * D),
        projector.reshape(2 * D, D),
        preferred_element_type=jnp.float32,
    )
    image_rows = (merge_terms + swap(merge_terms)).astype(jnp.bfloat16)

    per_peer = merged_count // seq_count
    run_starts = dest_positions.reshape(seq_count, merged_count)[:, 0]
    own_start = run_starts[seq_index]
    received = lax.all_to_all(
        jnp.roll(image_rows.reshape(per_peer, seq_count, image_rows.shape[1]), own_start, axis=1),
        "seq",
        split_axis=1,
        concat_axis=1,
        tiled=True,
    )
    slot_base = jnp.arange(per_peer, dtype=jnp.int32)[:, None] * seq_count
    landing = (
        run_starts[None, :] + slot_base + (seq_index - run_starts[None, :]) % seq_count
    ) // seq_count
    text_rows = text_embeds.shape[0]
    prompt = text_embeds.reshape(text_rows, D).at[landing.reshape(-1)].set(received.reshape(-1, D))
    text_normed = root_norm(prompt).astype(jnp.bfloat16)
    head_queries = root_norm(
        jnp.einsum(
            "td,dhe->hte",
            text_normed,
            decoder_q.reshape(D, local_heads, HEAD),
            preferred_element_type=jnp.float32,
        )
    ).astype(jnp.bfloat16)
    paired = jnp.dot(
        text_normed, decoder_kv.reshape(D, -1), preferred_element_type=jnp.float32
    ).reshape(text_rows, 2, HEAD)
    key_rows = root_norm(paired[:, 0]).astype(jnp.bfloat16)
    value_rows = paired[:, 1].astype(jnp.bfloat16)

    shared = jnp.stack([key_rows, value_rows], 0)[None]
    piece = lax.all_gather(shared, "seq", axis=0, tiled=True)
    rows = 32
    doc_starts = jnp.sum(
        (segment_ids[None] < jnp.arange(4, dtype=jnp.int32)[:, None, None]).astype(jnp.int32),
        (1, 2),
    )
    info = jnp.concatenate(
        [doc_starts, jnp.full((1,), seq_index, jnp.int32), jnp.zeros((3,), jnp.int32)]
    )
    decoder_out_full, head_queries = lax.optimization_barrier(
        (in_head_order(first, decoder_out, decoder_out_other, 0), head_queries)
    )
    head_major = text_attention(info, head_queries, piece, rows, scale)
    attended_text = jnp.transpose(head_major, (1, 0, 2)).reshape(text_rows, -1)
    all_heads = in_head_order(first, attended_text, swap(attended_text), 1)
    output_terms = jnp.dot(all_heads, decoder_out_full, preferred_element_type=jnp.float32)
    decoded = (prompt.astype(jnp.float32) + output_terms).astype(jnp.bfloat16)
    return decoded.reshape(text_rows, 1, D)


def solution(mesh):
    placed = (
        P("seq", None),
        P("seq", None),
        P("seq"),
        P(),
        P(None, "seq", None),
        P(),
        P(None, None, "section"),
        P("section", None),
        P("section", None, None),
        P(None, "section"),
        P(None, None, "section"),
        P("section", None),
    )
    return jax.shard_map(
        body, mesh=mesh, in_specs=placed, out_specs=P(None, "seq", None), check_vma=False
    )
```

```python
import math

import jax
import jax.numpy as jnp
from jax import lax
from jax.sharding import PartitionSpec as P
from jax.experimental import pallas as pl
from jax.experimental.pallas import tpu as pltpu
import functools

D = 1408
HEAD = 88


def layer_norm(values):
    values = values.astype(jnp.float32)
    centred = values - jnp.mean(values, -1, keepdims=True)
    return centred * lax.rsqrt(jnp.mean(centred * centred, -1, keepdims=True) + 1e-06)


def root_norm(values):
    values = values.astype(jnp.float32)
    return values * lax.rsqrt(jnp.mean(values * values, -1, keepdims=True) + 1e-06)


def merge_rows(grid, offsets, count):
    heights = grid[:, 0]
    widths = grid[:, 1]
    group_start = offsets // 4
    group_count = heights * widths // 4
    merged_ids = jnp.arange(count, dtype=jnp.int32)
    inside = (
        (merged_ids[:, None] >= group_start[None, :])
        & (merged_ids[:, None] < (group_start + group_count)[None, :])
    ).astype(jnp.int32)
    first_group = jnp.sum(inside * group_start[None, :], 1)
    first_patch = jnp.sum(inside * offsets[None, :], 1)
    row_width = jnp.sum(inside * widths[None, :], 1)
    within = merged_ids - first_group
    groups_across = row_width // 2
    group_row = within // groups_across
    group_col = within % groups_across
    corner = first_patch + 2 * group_row * row_width + 2 * group_col
    return jnp.stack([corner, corner + 1, corner + row_width, corner + row_width + 1], 1)


def _segment_start(info_ref, places):
    start = jnp.zeros_like(places) + info_ref[0]
    for doc in range(1, 4):
        bound = info_ref[doc]
        start = jnp.where(places >= bound, bound, start)
    return start


def _first_block(info_ref, qb, span):
    return _segment_start(info_ref, qb * span + info_ref[4]) // span


def _text_kernel(query_block_ref, key_block_ref, info_ref, q_ref, kv_ref, o_ref, acc_ref, tot_ref, *, scale):
    step = pl.program_id(0)
    qb = query_block_ref[step]
    kb = key_block_ref[step]
    heads, rows, head = q_ref.shape
    shards = kv_ref.shape[0]
    span = rows * shards
    own = info_ref[4]
    last_query = qb * span + own + (rows - 1) * shards
    active = kb >= _first_block(info_ref, qb, span)
    unmasked = (kb < qb) & (kb * span >= _segment_start(info_ref, last_query))

    @pl.when(kb == 0)
    def _():
        acc_ref[...] = jnp.zeros_like(acc_ref)
        tot_ref[...] = jnp.zeros_like(tot_ref)

    def accumulate(masked):
        q = q_ref[...].reshape(heads * rows, head)
        k = kv_ref[:, 0].reshape(span, head)
        v = kv_ref[:, 1].reshape(span, head)
        s = lax.dot_general(q, k, (((1,), (1,)), ((), ())), preferred_element_type=jnp.float32)
        w = jnp.exp(s * scale)
        if masked:
            row = lax.broadcasted_iota(jnp.int32, (heads * rows, 1), 0) & (rows - 1)
            query_places = (qb * rows + row) * shards + own
            lane = lax.broadcasted_iota(jnp.int32, (1, span), 1)
            key_places = (kb * rows + (lane & (rows - 1))) * shards + lax.shift_right_logical(
                lane, rows.bit_length() - 1
            )
            allowed = (key_places <= query_places) & (
                key_places >= _segment_start(info_ref, query_places)
            )
            w = jnp.where(allowed, w, 0.0)
        tot_ref[...] += jnp.sum(w, -1, keepdims=True)
        acc_ref[...] += jnp.dot(w.astype(jnp.bfloat16), v, preferred_element_type=jnp.float32)

    @pl.when(active & unmasked)
    def _():
        accumulate(False)

    @pl.when(active & jnp.logical_not(unmasked))
    def _():
        accumulate(True)

    @pl.when(kb == qb)
    def _():
        o_ref[...] = (acc_ref[...] / tot_ref[...]).astype(o_ref.dtype).reshape(o_ref.shape)


def text_attention(info, q, kv, rows, scale):
    heads, text_rows, head = q.shape
    shards = kv.shape[0]
    blocks = text_rows // rows
    span = rows * shards
    pairs = [(i, j) for i in range(blocks) for j in range(i + 1)]
    query_block = jnp.array([i for i, _ in pairs], jnp.int32)
    key_block = jnp.array([j for _, j in pairs], jnp.int32)

    def q_block(t, qb_ref, kb_ref, info_ref):
        return (0, qb_ref[t], 0)

    def kv_block(t, qb_ref, kb_ref, info_ref):
        qb = qb_ref[t]
        return (0, 0, jnp.maximum(kb_ref[t], _first_block(info_ref, qb, span)), 0)

    return pl.pallas_call(
        functools.partial(_text_kernel, scale=scale),
        grid_spec=pltpu.PrefetchScalarGridSpec(
            num_scalar_prefetch=3,
            grid=(len(pairs),),
            in_specs=[
                pl.BlockSpec((heads, rows, head), q_block),
                pl.BlockSpec((shards, 2, rows, head), kv_block),
            ],
            out_specs=pl.BlockSpec((heads, rows, head), q_block),
            scratch_shapes=[
                pltpu.VMEM((heads * rows, head), jnp.float32),
                pltpu.VMEM((heads * rows, 1), jnp.float32),
            ],
        ),
        out_shape=jax.ShapeDtypeStruct((heads, text_rows, head), jnp.bfloat16),
        compiler_params=pltpu.CompilerParams(dimension_semantics=("arbitrary",)),
    )(query_block, key_block, info, q, kv)


def swap(values):
    return lax.ppermute(values, "section", [(0, 1), (1, 0)])


def in_head_order(first, own, other, axis):
    return jnp.where(
        first, jnp.concatenate([own, other], axis), jnp.concatenate([other, own], axis)
    )


def body(
    patches,
    image_grid,
    image_offsets,
    dest_positions,
    text_embeds,
    segment_ids,
    vision_qkv,
    vision_out,
    projector,
    decoder_q,
    decoder_kv,
    decoder_out,
):
    section_index = lax.axis_index("section")
    seq_index = lax.axis_index("seq")
    seq_count = lax.axis_size("seq")
    first = section_index == 0
    scale = 3.0 / math.sqrt(HEAD)
    patch_count = patches.shape[0]
    local_heads = vision_out.shape[0] // HEAD
    merged_count = patch_count // 4

    vision_out_other = swap(vision_out)
    decoder_out_other = swap(decoder_out)

    normed = layer_norm(patches).astype(jnp.bfloat16)
    mixed = jnp.dot(normed, vision_qkv.reshape(D, -1), preferred_element_type=jnp.float32).reshape(
        patch_count, 3, local_heads, HEAD
    )
    queries = root_norm(mixed[:, 0]).astype(jnp.bfloat16)
    keys = root_norm(mixed[:, 1]).astype(jnp.bfloat16)
    values = mixed[:, 2].astype(jnp.bfloat16)
    offsets = image_offsets - seq_index * patch_count
    image_of = jnp.sum(
        (jnp.arange(patch_count, dtype=jnp.int32)[:, None] >= offsets[None, :]).astype(jnp.int32), 1
    )
    scores = jnp.einsum("qhd,khd->hqk", queries, keys, preferred_element_type=jnp.float32) * scale
    same = (image_of[:, None] == image_of[None, :])[None]
    weights = jnp.where(same, jnp.exp(scores), jnp.zeros_like(scores))
    totals = jnp.sum(weights, -1)
    mixed_values = jnp.einsum(
        "hqk,khd->qhd", weights.astype(jnp.bfloat16), values, preferred_element_type=jnp.float32
    )
    attended = (
        (mixed_values / jnp.transpose(totals)[:, :, None])
        .astype(jnp.bfloat16)
        .reshape(patch_count, local_heads * HEAD)
    )
    picks = merge_rows(image_grid, offsets, merged_count)
    own_picks = lax.dynamic_slice_in_dim(picks, 2 * section_index, 2, 1).reshape(-1)
    other_picks = lax.dynamic_slice_in_dim(picks, 2 - 2 * section_index, 2, 1).reshape(-1)
    patch_ids = jnp.arange(patch_count, dtype=jnp.int32)[None, :]
    own_select = (own_picks[:, None] == patch_ids).astype(jnp.bfloat16)
    other_select = (other_picks[:, None] == patch_ids).astype(jnp.bfloat16)
    received_heads = swap(
        jnp.dot(other_select, attended, preferred_element_type=jnp.float32).astype(jnp.bfloat16)
    )
    own_heads = jnp.dot(own_select, attended, preferred_element_type=jnp.float32).astype(
        jnp.bfloat16
    )
    own_rows = jnp.concatenate([own_heads, received_heads], 1)
    full_out = jnp.concatenate([vision_out, vision_out_other], 0)
    kept = (
        jnp.dot(own_select, patches, preferred_element_type=jnp.float32)
        + jnp.dot(own_rows, full_out, preferred_element_type=jnp.float32)
    ).astype(jnp.bfloat16)
    merge_terms = jnp.dot(
        kept.reshape(merged_count, 2 * D),
        projector.reshape(2 * D, D),
        preferred_element_type=jnp.float32,
    )
    image_rows = (merge_terms + swap(merge_terms)).astype(jnp.bfloat16)

    per_peer = merged_count // seq_count
    run_starts = dest_positions.reshape(seq_count, merged_count)[:, 0]
    own_start = run_starts[seq_index]
    received = lax.all_to_all(
        jnp.roll(image_rows.reshape(per_peer, seq_count, image_rows.shape[1]), own_start, axis=1),
        "seq",
        split_axis=1,
        concat_axis=1,
        tiled=True,
    )
    slot_base = jnp.arange(per_peer, dtype=jnp.int32)[:, None] * seq_count
    landing = (
        run_starts[None, :] + slot_base + (seq_index - run_starts[None, :]) % seq_count
    ) // seq_count
    text_rows = text_embeds.shape[0]
    prompt = text_embeds.reshape(text_rows, D).at[landing.reshape(-1)].set(received.reshape(-1, D))
    text_normed = root_norm(prompt).astype(jnp.bfloat16)
    head_queries = root_norm(
        jnp.einsum(
            "td,dhe->hte",
            text_normed,
            decoder_q.reshape(D, local_heads, HEAD),
            preferred_element_type=jnp.float32,
        )
    ).astype(jnp.bfloat16)
    paired = jnp.dot(
        text_normed, decoder_kv.reshape(D, -1), preferred_element_type=jnp.float32
    ).reshape(text_rows, 2, HEAD)
    key_rows = root_norm(paired[:, 0]).astype(jnp.bfloat16)
    value_rows = paired[:, 1].astype(jnp.bfloat16)

    shared = jnp.stack([key_rows, value_rows], 0).reshape(1, 2, text_rows * HEAD // 128, 128)
    piece = lax.all_gather(shared, "seq", axis=0, tiled=True).reshape(
        seq_count, 2, text_rows, HEAD
    )
    rows = 32
    doc_starts = jnp.sum(
        (segment_ids[None] < jnp.arange(4, dtype=jnp.int32)[:, None, None]).astype(jnp.int32),
        (1, 2),
    )
    info = jnp.concatenate(
        [doc_starts, jnp.full((1,), seq_index, jnp.int32), jnp.zeros((3,), jnp.int32)]
    )
    decoder_out_full, head_queries = lax.optimization_barrier(
        (in_head_order(first, decoder_out, decoder_out_other, 0), head_queries)
    )
    head_major = text_attention(info, head_queries, piece, rows, scale)
    attended_text = jnp.transpose(head_major, (1, 0, 2)).reshape(text_rows, -1)
    all_heads = in_head_order(first, attended_text, swap(attended_text), 1)
    output_terms = jnp.dot(all_heads, decoder_out_full, preferred_element_type=jnp.float32)
    decoded = (prompt.astype(jnp.float32) + output_terms).astype(jnp.bfloat16)
    return decoded.reshape(text_rows, 1, D)


def solution(mesh):
    placed = (
        P("seq", None),
        P("seq", None),
        P("seq"),
        P(),
        P(None, "seq", None),
        P(),
        P(None, None, "section"),
        P("section", None),
        P("section", None, None),
        P(None, "section"),
        P(None, None, "section"),
        P("section", None),
    )
    return jax.shard_map(
        body, mesh=mesh, in_specs=placed, out_specs=P(None, "seq", None), check_vma=False
    )
```

```python
import math

import jax
import jax.numpy as jnp
from jax import lax
from jax.sharding import PartitionSpec as P
from jax.experimental import pallas as pl
from jax.experimental.pallas import tpu as pltpu
import functools

D = 1408
HEAD = 88


def layer_norm(values):
    values = values.astype(jnp.float32)
    centred = values - jnp.mean(values, -1, keepdims=True)
    return centred * lax.rsqrt(jnp.mean(centred * centred, -1, keepdims=True) + 1e-06)


def root_norm(values):
    values = values.astype(jnp.float32)
    return values * lax.rsqrt(jnp.mean(values * values, -1, keepdims=True) + 1e-06)


def merge_rows(grid, offsets, count):
    heights = grid[:, 0]
    widths = grid[:, 1]
    group_start = offsets // 4
    group_count = heights * widths // 4
    merged_ids = jnp.arange(count, dtype=jnp.int32)
    inside = (
        (merged_ids[:, None] >= group_start[None, :])
        & (merged_ids[:, None] < (group_start + group_count)[None, :])
    ).astype(jnp.int32)
    first_group = jnp.sum(inside * group_start[None, :], 1)
    first_patch = jnp.sum(inside * offsets[None, :], 1)
    row_width = jnp.sum(inside * widths[None, :], 1)
    within = merged_ids - first_group
    groups_across = row_width // 2
    group_row = within // groups_across
    group_col = within % groups_across
    corner = first_patch + 2 * group_row * row_width + 2 * group_col
    return jnp.stack([corner, corner + 1, corner + row_width, corner + row_width + 1], 1)


def _segment_start(info_ref, places):
    start = jnp.zeros_like(places) + info_ref[0]
    for doc in range(1, 4):
        bound = info_ref[doc]
        start = jnp.where(places >= bound, bound, start)
    return start


def _first_block(info_ref, qb, span):
    return _segment_start(info_ref, qb * span + info_ref[4]) // span


def _text_kernel(query_block_ref, key_block_ref, info_ref, q_ref, kv_ref, o_ref, acc_ref, ext_ref, *, scale):
    step = pl.program_id(0)
    qb = query_block_ref[step]
    kb = key_block_ref[step]
    heads, rows, head = q_ref.shape
    shards = kv_ref.shape[0]
    span = rows * shards
    own = info_ref[4]
    last_query = qb * span + own + (rows - 1) * shards
    active = kb >= _first_block(info_ref, qb, span)
    unmasked = (kb < qb) & (kb * span >= _segment_start(info_ref, last_query))

    @pl.when(step == 0)
    def _():
        lane = lax.broadcasted_iota(jnp.int32, ext_ref.shape, 1)
        ext_ref[...] = jnp.where(lane == head, 1.0, 0.0).astype(ext_ref.dtype)

    @pl.when(kb == 0)
    def _():
        acc_ref[...] = jnp.zeros_like(acc_ref)

    def accumulate(masked):
        q = q_ref[...].reshape(heads * rows, head)
        k = kv_ref[:, 0].reshape(span, head)
        ext_ref[:, :head] = kv_ref[:, 1].reshape(span, head)
        s = lax.dot_general(q, k, (((1,), (1,)), ((), ())), preferred_element_type=jnp.float32)
        w = jnp.exp(s * scale)
        if masked:
            row = lax.broadcasted_iota(jnp.int32, (heads * rows, 1), 0) & (rows - 1)
            query_places = (qb * rows + row) * shards + own
            lane = lax.broadcasted_iota(jnp.int32, (1, span), 1)
            key_places = (kb * rows + (lane & (rows - 1))) * shards + lax.shift_right_logical(
                lane, rows.bit_length() - 1
            )
            allowed = (key_places <= query_places) & (
                key_places >= _segment_start(info_ref, query_places)
            )
            w = jnp.where(allowed, w, 0.0)
        acc_ref[...] += jnp.dot(
            w.astype(jnp.bfloat16), ext_ref[...], preferred_element_type=jnp.float32
        )

    @pl.when(active & unmasked)
    def _():
        accumulate(False)

    @pl.when(active & jnp.logical_not(unmasked))
    def _():
        accumulate(True)

    @pl.when(kb == qb)
    def _():
        acc = acc_ref[...]
        o_ref[...] = (acc[:, :head] / acc[:, head : head + 1]).astype(o_ref.dtype).reshape(
            o_ref.shape
        )


def text_attention(info, q, kv, rows, scale):
    heads, text_rows, head = q.shape
    shards = kv.shape[0]
    blocks = text_rows // rows
    span = rows * shards
    pairs = [(i, j) for i in range(blocks) for j in range(i + 1)]
    query_block = jnp.array([i for i, _ in pairs], jnp.int32)
    key_block = jnp.array([j for _, j in pairs], jnp.int32)

    def q_block(t, qb_ref, kb_ref, info_ref):
        return (0, qb_ref[t], 0)

    def kv_block(t, qb_ref, kb_ref, info_ref):
        qb = qb_ref[t]
        return (0, 0, jnp.maximum(kb_ref[t], _first_block(info_ref, qb, span)), 0)

    return pl.pallas_call(
        functools.partial(_text_kernel, scale=scale),
        grid_spec=pltpu.PrefetchScalarGridSpec(
            num_scalar_prefetch=3,
            grid=(len(pairs),),
            in_specs=[
                pl.BlockSpec((heads, rows, head), q_block),
                pl.BlockSpec((shards, 2, rows, head), kv_block),
            ],
            out_specs=pl.BlockSpec((heads, rows, head), q_block),
            scratch_shapes=[
                pltpu.VMEM((heads * rows, 128), jnp.float32),
                pltpu.VMEM((span, 128), jnp.bfloat16),
            ],
        ),
        out_shape=jax.ShapeDtypeStruct((heads, text_rows, head), jnp.bfloat16),
        compiler_params=pltpu.CompilerParams(dimension_semantics=("arbitrary",)),
    )(query_block, key_block, info, q, kv)


def swap(values):
    return lax.ppermute(values, "section", [(0, 1), (1, 0)])


def in_head_order(first, own, other, axis):
    return jnp.where(
        first, jnp.concatenate([own, other], axis), jnp.concatenate([other, own], axis)
    )


def body(
    patches,
    image_grid,
    image_offsets,
    dest_positions,
    text_embeds,
    segment_ids,
    vision_qkv,
    vision_out,
    projector,
    decoder_q,
    decoder_kv,
    decoder_out,
):
    section_index = lax.axis_index("section")
    seq_index = lax.axis_index("seq")
    seq_count = lax.axis_size("seq")
    first = section_index == 0
    scale = 3.0 / math.sqrt(HEAD)
    patch_count = patches.shape[0]
    local_heads = vision_out.shape[0] // HEAD
    merged_count = patch_count // 4

    vision_out_other = swap(vision_out)
    decoder_out_other = swap(decoder_out)

    normed = layer_norm(patches).astype(jnp.bfloat16)
    mixed = jnp.dot(normed, vision_qkv.reshape(D, -1), preferred_element_type=jnp.float32).reshape(
        patch_count, 3, local_heads, HEAD
    )
    queries = root_norm(mixed[:, 0]).astype(jnp.bfloat16)
    keys = root_norm(mixed[:, 1]).astype(jnp.bfloat16)
    values = mixed[:, 2].astype(jnp.bfloat16)
    offsets = image_offsets - seq_index * patch_count
    image_of = jnp.sum(
        (jnp.arange(patch_count, dtype=jnp.int32)[:, None] >= offsets[None, :]).astype(jnp.int32), 1
    )
    scores = jnp.einsum("qhd,khd->hqk", queries, keys, preferred_element_type=jnp.float32) * scale
    same = (image_of[:, None] == image_of[None, :])[None]
    weights = jnp.where(same, jnp.exp(scores), jnp.zeros_like(scores))
    totals = jnp.sum(weights, -1)
    mixed_values = jnp.einsum(
        "hqk,khd->qhd", weights.astype(jnp.bfloat16), values, preferred_element_type=jnp.float32
    )
    attended = (
        (mixed_values / jnp.transpose(totals)[:, :, None])
        .astype(jnp.bfloat16)
        .reshape(patch_count, local_heads * HEAD)
    )
    picks = merge_rows(image_grid, offsets, merged_count)
    own_picks = lax.dynamic_slice_in_dim(picks, 2 * section_index, 2, 1).reshape(-1)
    other_picks = lax.dynamic_slice_in_dim(picks, 2 - 2 * section_index, 2, 1).reshape(-1)
    patch_ids = jnp.arange(patch_count, dtype=jnp.int32)[None, :]
    own_select = (own_picks[:, None] == patch_ids).astype(jnp.bfloat16)
    other_select = (other_picks[:, None] == patch_ids).astype(jnp.bfloat16)
    received_heads = swap(
        jnp.dot(other_select, attended, preferred_element_type=jnp.float32).astype(jnp.bfloat16)
    )
    own_heads = jnp.dot(own_select, attended, preferred_element_type=jnp.float32).astype(
        jnp.bfloat16
    )
    own_rows = jnp.concatenate([own_heads, received_heads], 1)
    full_out = jnp.concatenate([vision_out, vision_out_other], 0)
    kept = (
        jnp.dot(own_select, patches, preferred_element_type=jnp.float32)
        + jnp.dot(own_rows, full_out, preferred_element_type=jnp.float32)
    ).astype(jnp.bfloat16)
    merge_terms = jnp.dot(
        kept.reshape(merged_count, 2 * D),
        projector.reshape(2 * D, D),
        preferred_element_type=jnp.float32,
    )
    image_rows = (merge_terms + swap(merge_terms)).astype(jnp.bfloat16)

    per_peer = merged_count // seq_count
    run_starts = dest_positions.reshape(seq_count, merged_count)[:, 0]
    own_start = run_starts[seq_index]
    received = lax.all_to_all(
        jnp.roll(image_rows.reshape(per_peer, seq_count, image_rows.shape[1]), own_start, axis=1),
        "seq",
        split_axis=1,
        concat_axis=1,
        tiled=True,
    )
    slot_base = jnp.arange(per_peer, dtype=jnp.int32)[:, None] * seq_count
    landing = (
        run_starts[None, :] + slot_base + (seq_index - run_starts[None, :]) % seq_count
    ) // seq_count
    text_rows = text_embeds.shape[0]
    prompt = text_embeds.reshape(text_rows, D).at[landing.reshape(-1)].set(received.reshape(-1, D))
    text_normed = root_norm(prompt).astype(jnp.bfloat16)
    head_queries = root_norm(
        jnp.einsum(
            "td,dhe->hte",
            text_normed,
            decoder_q.reshape(D, local_heads, HEAD),
            preferred_element_type=jnp.float32,
        )
    ).astype(jnp.bfloat16)
    paired = jnp.dot(
        text_normed, decoder_kv.reshape(D, -1), preferred_element_type=jnp.float32
    ).reshape(text_rows, 2, HEAD)
    key_rows = root_norm(paired[:, 0]).astype(jnp.bfloat16)
    value_rows = paired[:, 1].astype(jnp.bfloat16)

    shared = jnp.stack([key_rows, value_rows], 0)[None]
    piece = lax.all_gather(shared, "seq", axis=0, tiled=True)
    rows = 32
    doc_starts = jnp.sum(
        (segment_ids[None] < jnp.arange(4, dtype=jnp.int32)[:, None, None]).astype(jnp.int32),
        (1, 2),
    )
    info = jnp.concatenate(
        [doc_starts, jnp.full((1,), seq_index, jnp.int32), jnp.zeros((3,), jnp.int32)]
    )
    decoder_out_full, head_queries = lax.optimization_barrier(
        (in_head_order(first, decoder_out, decoder_out_other, 0), head_queries)
    )
    head_major = text_attention(info, head_queries, piece, rows, scale)
    attended_text = jnp.transpose(head_major, (1, 0, 2)).reshape(text_rows, -1)
    all_heads = in_head_order(first, attended_text, swap(attended_text), 1)
    output_terms = jnp.dot(all_heads, decoder_out_full, preferred_element_type=jnp.float32)
    decoded = (prompt.astype(jnp.float32) + output_terms).astype(jnp.bfloat16)
    return decoded.reshape(text_rows, 1, D)


def solution(mesh):
    placed = (
        P("seq", None),
        P("seq", None),
        P("seq"),
        P(),
        P(None, "seq", None),
        P(),
        P(None, None, "section"),
        P("section", None),
        P("section", None, None),
        P(None, "section"),
        P(None, None, "section"),
        P("section", None),
    )
    return jax.shard_map(
        body, mesh=mesh, in_specs=placed, out_specs=P(None, "seq", None), check_vma=False
    )
```

```python
import math

import jax
import jax.numpy as jnp
from jax import lax
from jax.sharding import PartitionSpec as P
from jax.experimental import pallas as pl
from jax.experimental.pallas import tpu as pltpu
import functools

D = 1408
HEAD = 88


def layer_norm(values):
    values = values.astype(jnp.float32)
    centred = values - jnp.mean(values, -1, keepdims=True)
    return centred * lax.rsqrt(jnp.mean(centred * centred, -1, keepdims=True) + 1e-06)


def root_norm(values):
    values = values.astype(jnp.float32)
    return values * lax.rsqrt(jnp.mean(values * values, -1, keepdims=True) + 1e-06)


def merge_rows(grid, offsets, count):
    heights = grid[:, 0]
    widths = grid[:, 1]
    group_start = offsets // 4
    group_count = heights * widths // 4
    merged_ids = jnp.arange(count, dtype=jnp.int32)
    inside = (
        (merged_ids[:, None] >= group_start[None, :])
        & (merged_ids[:, None] < (group_start + group_count)[None, :])
    ).astype(jnp.int32)
    first_group = jnp.sum(inside * group_start[None, :], 1)
    first_patch = jnp.sum(inside * offsets[None, :], 1)
    row_width = jnp.sum(inside * widths[None, :], 1)
    within = merged_ids - first_group
    groups_across = row_width // 2
    group_row = within // groups_across
    group_col = within % groups_across
    corner = first_patch + 2 * group_row * row_width + 2 * group_col
    return jnp.stack([corner, corner + 1, corner + row_width, corner + row_width + 1], 1)


def _segment_start(info_ref, places):
    start = jnp.zeros_like(places) + info_ref[0]
    for doc in range(1, 4):
        bound = info_ref[doc]
        start = jnp.where(places >= bound, bound, start)
    return start


def _text_kernel(plan_ref, fetch_ref, info_ref, q_ref, kv_ref, kpos_ref, o_ref, acc_ref, ext_ref, *, scale, blocks):
    qb = pl.program_id(0)
    kb = pl.program_id(1)
    heads, rows, head = q_ref.shape
    shards = kv_ref.shape[0]
    span = rows * shards
    own = info_ref[4]
    mode = plan_ref[qb * blocks + kb]

    @pl.when((qb == 0) & (kb == 0))
    def _():
        lane = lax.broadcasted_iota(jnp.int32, ext_ref.shape, 1)
        ext_ref[...] = jnp.where(lane == head, 1.0, 0.0).astype(ext_ref.dtype)

    @pl.when(kb == 0)
    def _():
        acc_ref[...] = jnp.zeros_like(acc_ref)

    def accumulate(masked):
        q = q_ref[...].reshape(heads * rows, head)
        k = kv_ref[:, 0].reshape(span, head)
        ext_ref[:, :head] = kv_ref[:, 1].reshape(span, head)
        s = lax.dot_general(q, k, (((1,), (1,)), ((), ())), preferred_element_type=jnp.float32)
        w = jnp.exp(s * scale)
        if masked:
            row = lax.broadcasted_iota(jnp.int32, (heads * rows, 1), 0) & (rows - 1)
            query_places = (qb * rows + row) * shards + own
            key_places = kpos_ref[0]
            allowed = (key_places <= query_places) & (
                key_places >= _segment_start(info_ref, query_places)
            )
            w = jnp.where(allowed, w, 0.0)
        acc_ref[...] += jnp.dot(
            w.astype(jnp.bfloat16), ext_ref[...], preferred_element_type=jnp.float32
        )

    @pl.when(mode == 1)
    def _():
        accumulate(False)

    @pl.when(mode == 2)
    def _():
        accumulate(True)

    @pl.when(kb == blocks - 1)
    def _():
        acc = acc_ref[...]
        o_ref[...] = (acc[:, :head] / acc[:, head : head + 1]).astype(o_ref.dtype).reshape(
            o_ref.shape
        )


def text_attention(info, q, kv, key_places, rows, scale):
    heads, text_rows, head = q.shape
    shards = kv.shape[0]
    blocks = text_rows // rows
    span = rows * shards
    block_places = jnp.transpose(key_places.reshape(shards, blocks, rows), (1, 0, 2)).reshape(
        blocks, 1, span
    )
    lowest = jnp.min(block_places, (1, 2))
    highest = jnp.max(block_places, (1, 2))
    first_query = jnp.arange(blocks, dtype=jnp.int32) * span + info[4]
    last_query = first_query + (rows - 1) * shards

    def segment_start(places):
        start = jnp.zeros_like(places) + info[0]
        for doc in range(1, 4):
            start = jnp.where(places >= info[doc], info[doc], start)
        return start

    active = (lowest[None, :] <= last_query[:, None]) & (
        highest[None, :] >= segment_start(first_query)[:, None]
    )
    clear = (highest[None, :] <= first_query[:, None]) & (
        lowest[None, :] >= segment_start(last_query)[:, None]
    )
    plan = jnp.where(active, jnp.where(clear, 1, 2), 0).astype(jnp.int32)
    key_ids = jnp.broadcast_to(jnp.arange(blocks, dtype=jnp.int32)[None, :], (blocks, blocks))
    seen = lax.cummax(jnp.where(active, key_ids, -1), axis=1)
    first_active = jnp.argmax(active, axis=1).astype(jnp.int32)
    fetch = jnp.where(seen < 0, first_active[:, None], seen).astype(jnp.int32)

    def q_block(i, j, plan_ref, fetch_ref, info_ref):
        return (0, i, 0)

    def kv_block(i, j, plan_ref, fetch_ref, info_ref):
        return (0, 0, fetch_ref[i * blocks + j], 0)

    def kpos_block(i, j, plan_ref, fetch_ref, info_ref):
        return (fetch_ref[i * blocks + j], 0, 0)

    return pl.pallas_call(
        functools.partial(_text_kernel, scale=scale, blocks=blocks),
        grid_spec=pltpu.PrefetchScalarGridSpec(
            num_scalar_prefetch=3,
            grid=(blocks, blocks),
            in_specs=[
                pl.BlockSpec((heads, rows, head), q_block),
                pl.BlockSpec((shards, 2, rows, head), kv_block),
                pl.BlockSpec((1, 1, span), kpos_block),
            ],
            out_specs=pl.BlockSpec((heads, rows, head), q_block),
            scratch_shapes=[
                pltpu.VMEM((heads * rows, 128), jnp.float32),
                pltpu.VMEM((span, 128), jnp.bfloat16),
            ],
        ),
        out_shape=jax.ShapeDtypeStruct((heads, text_rows, head), jnp.bfloat16),
        compiler_params=pltpu.CompilerParams(dimension_semantics=("arbitrary", "arbitrary")),
    )(plan.reshape(-1), fetch.reshape(-1), info, q, kv, block_places)


def swap(values):
    return lax.ppermute(values, "section", [(0, 1), (1, 0)])


def in_head_order(first, own, other, axis):
    return jnp.where(
        first, jnp.concatenate([own, other], axis), jnp.concatenate([other, own], axis)
    )


def body(
    patches,
    image_grid,
    image_offsets,
    dest_positions,
    text_embeds,
    segment_ids,
    vision_qkv,
    vision_out,
    projector,
    decoder_q,
    decoder_kv,
    decoder_out,
):
    section_index = lax.axis_index("section")
    seq_index = lax.axis_index("seq")
    seq_count = lax.axis_size("seq")
    first = section_index == 0
    scale = 3.0 / math.sqrt(HEAD)
    patch_count = patches.shape[0]
    local_heads = vision_out.shape[0] // HEAD
    merged_count = patch_count // 4

    vision_out_other = swap(vision_out)
    decoder_out_other = swap(decoder_out)

    normed = layer_norm(patches).astype(jnp.bfloat16)
    mixed = jnp.dot(normed, vision_qkv.reshape(D, -1), preferred_element_type=jnp.float32).reshape(
        patch_count, 3, local_heads, HEAD
    )
    queries = root_norm(mixed[:, 0]).astype(jnp.bfloat16)
    keys = root_norm(mixed[:, 1]).astype(jnp.bfloat16)
    values = mixed[:, 2].astype(jnp.bfloat16)
    offsets = image_offsets - seq_index * patch_count
    image_of = jnp.sum(
        (jnp.arange(patch_count, dtype=jnp.int32)[:, None] >= offsets[None, :]).astype(jnp.int32), 1
    )
    scores = jnp.einsum("qhd,khd->hqk", queries, keys, preferred_element_type=jnp.float32) * scale
    same = (image_of[:, None] == image_of[None, :])[None]
    weights = jnp.where(same, jnp.exp(scores), jnp.zeros_like(scores))
    totals = jnp.sum(weights, -1)
    mixed_values = jnp.einsum(
        "hqk,khd->qhd", weights.astype(jnp.bfloat16), values, preferred_element_type=jnp.float32
    )
    attended = (
        (mixed_values / jnp.transpose(totals)[:, :, None])
        .astype(jnp.bfloat16)
        .reshape(patch_count, local_heads * HEAD)
    )
    picks = merge_rows(image_grid, offsets, merged_count)
    own_picks = lax.dynamic_slice_in_dim(picks, 2 * section_index, 2, 1).reshape(-1)
    other_picks = lax.dynamic_slice_in_dim(picks, 2 - 2 * section_index, 2, 1).reshape(-1)
    patch_ids = jnp.arange(patch_count, dtype=jnp.int32)[None, :]
    own_select = (own_picks[:, None] == patch_ids).astype(jnp.bfloat16)
    other_select = (other_picks[:, None] == patch_ids).astype(jnp.bfloat16)
    received_heads = swap(
        jnp.dot(other_select, attended, preferred_element_type=jnp.float32).astype(jnp.bfloat16)
    )
    own_heads = jnp.dot(own_select, attended, preferred_element_type=jnp.float32).astype(
        jnp.bfloat16
    )
    own_rows = jnp.concatenate([own_heads, received_heads], 1)
    full_out = jnp.concatenate([vision_out, vision_out_other], 0)
    kept = (
        jnp.dot(own_select, patches, preferred_element_type=jnp.float32)
        + jnp.dot(own_rows, full_out, preferred_element_type=jnp.float32)
    ).astype(jnp.bfloat16)
    merge_terms = jnp.dot(
        kept.reshape(merged_count, 2 * D),
        projector.reshape(2 * D, D),
        preferred_element_type=jnp.float32,
    )
    image_rows = (merge_terms + swap(merge_terms)).astype(jnp.bfloat16)

    def key_value(rows_in):
        normed_rows = root_norm(rows_in).astype(jnp.bfloat16)
        paired = jnp.dot(
            normed_rows, decoder_kv.reshape(D, -1), preferred_element_type=jnp.float32
        ).reshape(rows_in.shape[0], 2, HEAD)
        return jnp.stack(
            [root_norm(paired[:, 0]).astype(jnp.bfloat16), paired[:, 1].astype(jnp.bfloat16)], 0
        )

    text_rows = text_embeds.shape[0]
    run_starts = dest_positions.reshape(seq_count, merged_count)[:, 0]
    places = (
        jnp.arange(text_rows, dtype=jnp.int32)[:, None] * seq_count
        + jnp.arange(seq_count, dtype=jnp.int32)[None, :]
    )
    is_text = jnp.logical_not(
        jnp.any(
            (places[..., None] >= run_starts) & (places[..., None] < run_starts + merged_count), -1
        )
    )
    text_rank = jnp.cumsum(is_text.astype(jnp.int32), 0) - 1
    slots = jnp.arange(merged_count, dtype=jnp.int32)
    text_pick = (text_rank[None] == slots[:, None, None]) & is_text[None]
    text_places = jnp.sum(jnp.where(text_pick, places[None], 0), 1).T
    own_pick = lax.dynamic_slice_in_dim(text_pick, seq_index, 1, 2)[:, :, 0]
    text_kv = jnp.einsum(
        "ci,kid->kcd",
        own_pick.astype(jnp.bfloat16),
        key_value(text_embeds.reshape(text_rows, D)),
        preferred_element_type=jnp.float32,
    ).astype(jnp.bfloat16)
    contribution = jnp.concatenate([text_kv, key_value(image_rows)], 1)[None]
    piece = lax.all_gather(contribution, "seq", axis=0, tiled=True)
    order = jnp.argsort(run_starts)
    sorted_starts = run_starts[order]
    all_kv = jnp.concatenate(
        [piece[:, :, :merged_count], jnp.take(piece[:, :, merged_count:], order, axis=0)], 2
    )
    all_places = jnp.concatenate([text_places, sorted_starts[:, None] + slots[None, :]], 1)

    per_peer = merged_count // seq_count
    own_start = run_starts[seq_index]
    received = lax.all_to_all(
        jnp.roll(image_rows.reshape(per_peer, seq_count, image_rows.shape[1]), own_start, axis=1),
        "seq",
        split_axis=1,
        concat_axis=1,
        tiled=True,
    )
    slot_base = jnp.arange(per_peer, dtype=jnp.int32)[:, None] * seq_count
    landing = (
        run_starts[None, :] + slot_base + (seq_index - run_starts[None, :]) % seq_count
    ) // seq_count
    prompt = text_embeds.reshape(text_rows, D).at[landing.reshape(-1)].set(received.reshape(-1, D))
    text_normed = root_norm(prompt).astype(jnp.bfloat16)
    head_queries = root_norm(
        jnp.einsum(
            "td,dhe->hte",
            text_normed,
            decoder_q.reshape(D, local_heads, HEAD),
            preferred_element_type=jnp.float32,
        )
    ).astype(jnp.bfloat16)
    rows = 32
    doc_starts = jnp.sum(
        (segment_ids[None] < jnp.arange(4, dtype=jnp.int32)[:, None, None]).astype(jnp.int32),
        (1, 2),
    )
    info = jnp.concatenate(
        [doc_starts, jnp.full((1,), seq_index, jnp.int32), jnp.zeros((3,), jnp.int32)]
    )
    decoder_out_full, head_queries = lax.optimization_barrier(
        (in_head_order(first, decoder_out, decoder_out_other, 0), head_queries)
    )
    head_major = text_attention(info, head_queries, all_kv, all_places, rows, scale)
    attended_text = jnp.transpose(head_major, (1, 0, 2)).reshape(text_rows, -1)
    all_heads = in_head_order(first, attended_text, swap(attended_text), 1)
    output_terms = jnp.dot(all_heads, decoder_out_full, preferred_element_type=jnp.float32)
    decoded = (prompt.astype(jnp.float32) + output_terms).astype(jnp.bfloat16)
    return decoded.reshape(text_rows, 1, D)


def solution(mesh):
    placed = (
        P("seq", None),
        P("seq", None),
        P("seq"),
        P(),
        P(None, "seq", None),
        P(),
        P(None, None, "section"),
        P("section", None),
        P("section", None, None),
        P(None, "section"),
        P(None, None, "section"),
        P("section", None),
    )
    return jax.shard_map(
        body, mesh=mesh, in_specs=placed, out_specs=P(None, "seq", None), check_vma=False
    )
```

```python
import math

import jax
import jax.numpy as jnp
from jax import lax
from jax.sharding import PartitionSpec as P
from jax.experimental import pallas as pl
from jax.experimental.pallas import tpu as pltpu
import functools

D = 1408
HEAD = 88


def layer_norm(values):
    values = values.astype(jnp.float32)
    centred = values - jnp.mean(values, -1, keepdims=True)
    return centred * lax.rsqrt(jnp.mean(centred * centred, -1, keepdims=True) + 1e-06)


def root_norm(values):
    values = values.astype(jnp.float32)
    return values * lax.rsqrt(jnp.mean(values * values, -1, keepdims=True) + 1e-06)


def merge_rows(grid, offsets, count):
    heights = grid[:, 0]
    widths = grid[:, 1]
    group_start = offsets // 4
    group_count = heights * widths // 4
    merged_ids = jnp.arange(count, dtype=jnp.int32)
    inside = (
        (merged_ids[:, None] >= group_start[None, :])
        & (merged_ids[:, None] < (group_start + group_count)[None, :])
    ).astype(jnp.int32)
    first_group = jnp.sum(inside * group_start[None, :], 1)
    first_patch = jnp.sum(inside * offsets[None, :], 1)
    row_width = jnp.sum(inside * widths[None, :], 1)
    within = merged_ids - first_group
    groups_across = row_width // 2
    group_row = within // groups_across
    group_col = within % groups_across
    corner = first_patch + 2 * group_row * row_width + 2 * group_col
    return jnp.stack([corner, corner + 1, corner + row_width, corner + row_width + 1], 1)


def _segment_start(info_ref, places):
    start = jnp.zeros_like(places) + info_ref[0]
    for doc in range(1, 4):
        bound = info_ref[doc]
        start = jnp.where(places >= bound, bound, start)
    return start


def _first_block(info_ref, qb, span):
    return _segment_start(info_ref, qb * span + info_ref[4]) // span


def _text_kernel(query_block_ref, key_block_ref, info_ref, q_ref, kv_ref, o_ref, acc_ref, ext_ref, *, scale):
    step = pl.program_id(0)
    qb = query_block_ref[step]
    kb = key_block_ref[step]
    heads, rows, head = q_ref.shape
    shards = kv_ref.shape[0]
    span = rows * shards
    own = info_ref[4]
    last_query = qb * span + own + (rows - 1) * shards
    active = kb >= _first_block(info_ref, qb, span)
    unmasked = (kb < qb) & (kb * span >= _segment_start(info_ref, last_query))

    @pl.when(step == 0)
    def _():
        lane = lax.broadcasted_iota(jnp.int32, ext_ref.shape, 1)
        ext_ref[...] = jnp.where(lane == head, 1.0, 0.0).astype(ext_ref.dtype)

    @pl.when(kb == 0)
    def _():
        acc_ref[...] = jnp.zeros_like(acc_ref)

    def accumulate(masked):
        q = q_ref[...].reshape(heads * rows, head)
        k = kv_ref[:, 0].reshape(span, head)
        ext_ref[:, :head] = kv_ref[:, 1].reshape(span, head)
        s = lax.dot_general(q, k, (((1,), (1,)), ((), ())), preferred_element_type=jnp.float32)
        w = jnp.exp(s * scale)
        if masked:
            row = lax.broadcasted_iota(jnp.int32, (heads * rows, 1), 0) & (rows - 1)
            query_places = (qb * rows + row) * shards + own
            lane = lax.broadcasted_iota(jnp.int32, (1, span), 1)
            key_places = (kb * rows + (lane & (rows - 1))) * shards + lax.shift_right_logical(
                lane, rows.bit_length() - 1
            )
            allowed = (key_places <= query_places) & (
                key_places >= _segment_start(info_ref, query_places)
            )
            w = jnp.where(allowed, w, 0.0)
        acc_ref[...] += jnp.dot(
            w.astype(jnp.bfloat16), ext_ref[...], preferred_element_type=jnp.float32
        )

    @pl.when(active & unmasked)
    def _():
        accumulate(False)

    @pl.when(active & jnp.logical_not(unmasked))
    def _():
        accumulate(True)

    @pl.when(kb == qb)
    def _():
        acc = acc_ref[...]
        o_ref[...] = (acc[:, :head] / acc[:, head : head + 1]).astype(o_ref.dtype).reshape(
            o_ref.shape
        )


def text_attention(info, q, kv, rows, scale):
    heads, text_rows, head = q.shape
    shards = kv.shape[0]
    blocks = text_rows // rows
    span = rows * shards
    pairs = [(i, j) for i in range(blocks) for j in range(i + 1)]
    query_block = jnp.array([i for i, _ in pairs], jnp.int32)
    key_block = jnp.array([j for _, j in pairs], jnp.int32)

    def q_block(t, qb_ref, kb_ref, info_ref):
        return (0, qb_ref[t], 0)

    def kv_block(t, qb_ref, kb_ref, info_ref):
        qb = qb_ref[t]
        return (0, 0, jnp.maximum(kb_ref[t], _first_block(info_ref, qb, span)), 0)

    return pl.pallas_call(
        functools.partial(_text_kernel, scale=scale),
        grid_spec=pltpu.PrefetchScalarGridSpec(
            num_scalar_prefetch=3,
            grid=(len(pairs),),
            in_specs=[
                pl.BlockSpec((heads, rows, head), q_block),
                pl.BlockSpec((shards, 2, rows, head), kv_block),
            ],
            out_specs=pl.BlockSpec((heads, rows, head), q_block),
            scratch_shapes=[
                pltpu.VMEM((heads * rows, 128), jnp.float32),
                pltpu.VMEM((span, 128), jnp.bfloat16),
            ],
        ),
        out_shape=jax.ShapeDtypeStruct((heads, text_rows, head), jnp.bfloat16),
        compiler_params=pltpu.CompilerParams(dimension_semantics=("arbitrary",)),
    )(query_block, key_block, info, q, kv)


def swap(values):
    return lax.ppermute(values, "section", [(0, 1), (1, 0)])


def in_head_order(first, own, other, axis):
    return jnp.where(
        first, jnp.concatenate([own, other], axis), jnp.concatenate([other, own], axis)
    )


def body(
    patches,
    image_grid,
    image_offsets,
    dest_positions,
    text_embeds,
    segment_ids,
    vision_qkv,
    vision_out,
    projector,
    decoder_q,
    decoder_kv,
    decoder_out,
):
    section_index = lax.axis_index("section")
    seq_index = lax.axis_index("seq")
    seq_count = lax.axis_size("seq")
    first = section_index == 0
    scale = 3.0 / math.sqrt(HEAD)
    patch_count = patches.shape[0]
    local_heads = vision_out.shape[0] // HEAD
    merged_count = patch_count // 4

    vision_out_other = swap(vision_out)
    decoder_out_other = swap(decoder_out)

    normed = layer_norm(patches).astype(jnp.bfloat16)
    mixed = jnp.dot(normed, vision_qkv.reshape(D, -1), preferred_element_type=jnp.float32).reshape(
        patch_count, 3, local_heads, HEAD
    )
    queries = root_norm(mixed[:, 0]).astype(jnp.bfloat16)
    keys = root_norm(mixed[:, 1]).astype(jnp.bfloat16)
    values = mixed[:, 2].astype(jnp.bfloat16)
    offsets = image_offsets - seq_index * patch_count
    image_of = jnp.sum(
        (jnp.arange(patch_count, dtype=jnp.int32)[:, None] >= offsets[None, :]).astype(jnp.int32), 1
    )
    scores = jnp.einsum("qhd,khd->hqk", queries, keys, preferred_element_type=jnp.float32) * scale
    same = (image_of[:, None] == image_of[None, :])[None]
    weights = jnp.where(same, jnp.exp(scores), jnp.zeros_like(scores))
    totals = jnp.sum(weights, -1)
    mixed_values = jnp.einsum(
        "hqk,khd->qhd", weights.astype(jnp.bfloat16), values, preferred_element_type=jnp.float32
    )
    attended = (
        (mixed_values / jnp.transpose(totals)[:, :, None])
        .astype(jnp.bfloat16)
        .reshape(patch_count, local_heads * HEAD)
    )
    picks = merge_rows(image_grid, offsets, merged_count)
    own_picks = lax.dynamic_slice_in_dim(picks, 2 * section_index, 2, 1).reshape(-1)
    other_picks = lax.dynamic_slice_in_dim(picks, 2 - 2 * section_index, 2, 1).reshape(-1)
    patch_ids = jnp.arange(patch_count, dtype=jnp.int32)[None, :]
    own_select = (own_picks[:, None] == patch_ids).astype(jnp.bfloat16)
    other_select = (other_picks[:, None] == patch_ids).astype(jnp.bfloat16)
    received_heads = swap(
        jnp.dot(other_select, attended, preferred_element_type=jnp.float32).astype(jnp.bfloat16)
    )
    own_heads = jnp.dot(own_select, attended, preferred_element_type=jnp.float32).astype(
        jnp.bfloat16
    )
    own_rows = jnp.concatenate([own_heads, received_heads], 1)
    full_out = jnp.concatenate([vision_out, vision_out_other], 0)
    kept = (
        jnp.dot(own_select, patches, preferred_element_type=jnp.float32)
        + jnp.dot(own_rows, full_out, preferred_element_type=jnp.float32)
    ).astype(jnp.bfloat16)
    merge_terms = jnp.dot(
        kept.reshape(merged_count, 2 * D),
        projector.reshape(2 * D, D),
        preferred_element_type=jnp.float32,
    )
    image_rows = (merge_terms + swap(merge_terms)).astype(jnp.bfloat16)

    per_peer = merged_count // seq_count
    run_starts = dest_positions.reshape(seq_count, merged_count)[:, 0]
    own_start = run_starts[seq_index]
    received = lax.all_to_all(
        jnp.roll(image_rows.reshape(per_peer, seq_count, image_rows.shape[1]), own_start, axis=1),
        "seq",
        split_axis=1,
        concat_axis=1,
        tiled=True,
    )
    slot_base = jnp.arange(per_peer, dtype=jnp.int32)[:, None] * seq_count
    landing = (
        run_starts[None, :] + slot_base + (seq_index - run_starts[None, :]) % seq_count
    ) // seq_count
    text_rows = text_embeds.shape[0]
    prompt = text_embeds.reshape(text_rows, D).at[landing.reshape(-1)].set(received.reshape(-1, D))
    text_normed = root_norm(prompt).astype(jnp.bfloat16)
    head_queries = root_norm(
        jnp.einsum(
            "td,dhe->hte",
            text_normed,
            decoder_q.reshape(D, local_heads, HEAD),
            preferred_element_type=jnp.float32,
        )
    ).astype(jnp.bfloat16)
    paired = jnp.dot(
        text_normed, decoder_kv.reshape(D, -1), preferred_element_type=jnp.float32
    ).reshape(text_rows, 2, HEAD)
    key_rows = root_norm(paired[:, 0]).astype(jnp.bfloat16)
    value_rows = paired[:, 1].astype(jnp.bfloat16)

    shared = jnp.stack([key_rows, value_rows], 0)[None]
    piece = lax.all_gather(shared, "seq", axis=0, tiled=True)
    rows = 64
    doc_starts = jnp.sum(
        (segment_ids[None] < jnp.arange(4, dtype=jnp.int32)[:, None, None]).astype(jnp.int32),
        (1, 2),
    )
    info = jnp.concatenate(
        [doc_starts, jnp.full((1,), seq_index, jnp.int32), jnp.zeros((3,), jnp.int32)]
    )
    decoder_out_full, head_queries = lax.optimization_barrier(
        (in_head_order(first, decoder_out, decoder_out_other, 0), head_queries)
    )
    head_major = text_attention(info, head_queries, piece, rows, scale)
    attended_text = jnp.transpose(head_major, (1, 0, 2)).reshape(text_rows, -1)
    all_heads = in_head_order(first, attended_text, swap(attended_text), 1)
    output_terms = jnp.dot(all_heads, decoder_out_full, preferred_element_type=jnp.float32)
    decoded = (prompt.astype(jnp.float32) + output_terms).astype(jnp.bfloat16)
    return decoded.reshape(text_rows, 1, D)


def solution(mesh):
    placed = (
        P("seq", None),
        P("seq", None),
        P("seq"),
        P(),
        P(None, "seq", None),
        P(),
        P(None, None, "section"),
        P("section", None),
        P("section", None, None),
        P(None, "section"),
        P(None, None, "section"),
        P("section", None),
    )
    return jax.shard_map(
        body, mesh=mesh, in_specs=placed, out_specs=P(None, "seq", None), check_vma=False
    )
```

```python
import math

import jax
import jax.numpy as jnp
from jax import lax
from jax.sharding import PartitionSpec as P
from jax.experimental import pallas as pl
from jax.experimental.pallas import tpu as pltpu
import functools

D = 1408
HEAD = 88


def layer_norm(values):
    values = values.astype(jnp.float32)
    centred = values - jnp.mean(values, -1, keepdims=True)
    return centred * lax.rsqrt(jnp.mean(centred * centred, -1, keepdims=True) + 1e-06)


def root_norm(values):
    values = values.astype(jnp.float32)
    return values * lax.rsqrt(jnp.mean(values * values, -1, keepdims=True) + 1e-06)


def merge_rows(grid, offsets, count):
    heights = grid[:, 0]
    widths = grid[:, 1]
    group_start = offsets // 4
    group_count = heights * widths // 4
    merged_ids = jnp.arange(count, dtype=jnp.int32)
    inside = (
        (merged_ids[:, None] >= group_start[None, :])
        & (merged_ids[:, None] < (group_start + group_count)[None, :])
    ).astype(jnp.int32)
    first_group = jnp.sum(inside * group_start[None, :], 1)
    first_patch = jnp.sum(inside * offsets[None, :], 1)
    row_width = jnp.sum(inside * widths[None, :], 1)
    within = merged_ids - first_group
    groups_across = row_width // 2
    group_row = within // groups_across
    group_col = within % groups_across
    corner = first_patch + 2 * group_row * row_width + 2 * group_col
    return jnp.stack([corner, corner + 1, corner + row_width, corner + row_width + 1], 1)


def _segment_start(info_ref, places):
    start = jnp.zeros_like(places) + info_ref[0]
    for doc in range(1, 4):
        bound = info_ref[doc]
        start = jnp.where(places >= bound, bound, start)
    return start


def _first_block(info_ref, qb, span):
    return _segment_start(info_ref, qb * span + info_ref[4]) // span


def _text_kernel(query_block_ref, key_block_ref, info_ref, q_ref, kv_ref, o_ref, acc_ref, ext_ref, *, scale):
    step = pl.program_id(0)
    qb = query_block_ref[step]
    kb = key_block_ref[step]
    heads, rows, head = q_ref.shape
    shards = kv_ref.shape[0]
    span = rows * shards
    own = info_ref[4]
    last_query = qb * span + own + (rows - 1) * shards
    active = kb >= _first_block(info_ref, qb, span)
    unmasked = (kb < qb) & (kb * span >= _segment_start(info_ref, last_query))

    @pl.when(step == 0)
    def _():
        lane = lax.broadcasted_iota(jnp.int32, ext_ref.shape, 1)
        ext_ref[...] = jnp.where(lane == head, 1.0, 0.0).astype(ext_ref.dtype)

    @pl.when(kb == 0)
    def _():
        acc_ref[...] = jnp.zeros_like(acc_ref)

    def accumulate(masked):
        q = q_ref[...].reshape(heads * rows, head)
        k = kv_ref[:, 0].reshape(span, head)
        ext_ref[:, :head] = kv_ref[:, 1].reshape(span, head)
        s = lax.dot_general(q, k, (((1,), (1,)), ((), ())), preferred_element_type=jnp.float32)
        w = jnp.exp(s * scale)
        if masked:
            row = lax.broadcasted_iota(jnp.int32, (heads * rows, 1), 0) & (rows - 1)
            query_places = (qb * rows + row) * shards + own
            lane = lax.broadcasted_iota(jnp.int32, (1, span), 1)
            key_places = (kb * rows + (lane & (rows - 1))) * shards + lax.shift_right_logical(
                lane, rows.bit_length() - 1
            )
            allowed = (key_places <= query_places) & (
                key_places >= _segment_start(info_ref, query_places)
            )
            w = jnp.where(allowed, w, 0.0)
        acc_ref[...] += jnp.dot(
            w.astype(jnp.bfloat16), ext_ref[...], preferred_element_type=jnp.float32
        )

    @pl.when(active & unmasked)
    def _():
        accumulate(False)

    @pl.when(active & jnp.logical_not(unmasked))
    def _():
        accumulate(True)

    @pl.when(kb == qb)
    def _():
        acc = acc_ref[...]
        o_ref[...] = (acc[:, :head] / acc[:, head : head + 1]).astype(o_ref.dtype).reshape(
            o_ref.shape
        )


def text_attention(info, q, kv, rows, scale):
    heads, text_rows, head = q.shape
    shards = kv.shape[0]
    blocks = text_rows // rows
    span = rows * shards
    pairs = [(i, j) for i in range(blocks) for j in range(i + 1)]
    query_block = jnp.array([i for i, _ in pairs], jnp.int32)
    key_block = jnp.array([j for _, j in pairs], jnp.int32)

    def q_block(t, qb_ref, kb_ref, info_ref):
        return (0, qb_ref[t], 0)

    def kv_block(t, qb_ref, kb_ref, info_ref):
        qb = qb_ref[t]
        return (0, 0, jnp.maximum(kb_ref[t], _first_block(info_ref, qb, span)), 0)

    return pl.pallas_call(
        functools.partial(_text_kernel, scale=scale),
        grid_spec=pltpu.PrefetchScalarGridSpec(
            num_scalar_prefetch=3,
            grid=(len(pairs),),
            in_specs=[
                pl.BlockSpec((heads, rows, head), q_block),
                pl.BlockSpec((shards, 2, rows, head), kv_block),
            ],
            out_specs=pl.BlockSpec((heads, rows, head), q_block),
            scratch_shapes=[
                pltpu.VMEM((heads * rows, 128), jnp.float32),
                pltpu.VMEM((span, 128), jnp.bfloat16),
            ],
        ),
        out_shape=jax.ShapeDtypeStruct((heads, text_rows, head), jnp.bfloat16),
        compiler_params=pltpu.CompilerParams(dimension_semantics=("arbitrary",)),
    )(query_block, key_block, info, q, kv)


def swap(values):
    return lax.ppermute(values, "section", [(0, 1), (1, 0)])


def in_head_order(first, own, other, axis):
    return jnp.where(
        first, jnp.concatenate([own, other], axis), jnp.concatenate([other, own], axis)
    )


def body(
    patches,
    image_grid,
    image_offsets,
    dest_positions,
    text_embeds,
    segment_ids,
    vision_qkv,
    vision_out,
    projector,
    decoder_q,
    decoder_kv,
    decoder_out,
):
    section_index = lax.axis_index("section")
    seq_index = lax.axis_index("seq")
    seq_count = lax.axis_size("seq")
    first = section_index == 0
    scale = 3.0 / math.sqrt(HEAD)
    patch_count = patches.shape[0]
    local_heads = vision_out.shape[0] // HEAD
    merged_count = patch_count // 4

    vision_out_other = swap(vision_out)
    decoder_out_other = swap(decoder_out)

    normed = layer_norm(patches).astype(jnp.bfloat16)
    mixed = jnp.dot(normed, vision_qkv.reshape(D, -1), preferred_element_type=jnp.float32).reshape(
        patch_count, 3, local_heads, HEAD
    )
    queries = root_norm(mixed[:, 0]).astype(jnp.bfloat16)
    keys = root_norm(mixed[:, 1]).astype(jnp.bfloat16)
    values = mixed[:, 2].astype(jnp.bfloat16)
    offsets = image_offsets - seq_index * patch_count
    image_of = jnp.sum(
        (jnp.arange(patch_count, dtype=jnp.int32)[:, None] >= offsets[None, :]).astype(jnp.int32), 1
    )
    scores = jnp.einsum("qhd,khd->hqk", queries, keys, preferred_element_type=jnp.float32) * scale
    same = (image_of[:, None] == image_of[None, :])[None]
    weights = jnp.where(same, jnp.exp(scores), jnp.zeros_like(scores))
    totals = jnp.sum(weights, -1)
    mixed_values = jnp.einsum(
        "hqk,khd->qhd", weights.astype(jnp.bfloat16), values, preferred_element_type=jnp.float32
    )
    attended = (
        (mixed_values / jnp.transpose(totals)[:, :, None])
        .astype(jnp.bfloat16)
        .reshape(patch_count, local_heads * HEAD)
    )
    picks = merge_rows(image_grid, offsets, merged_count)
    own_picks = lax.dynamic_slice_in_dim(picks, 2 * section_index, 2, 1).reshape(-1)
    other_picks = lax.dynamic_slice_in_dim(picks, 2 - 2 * section_index, 2, 1).reshape(-1)
    patch_ids = jnp.arange(patch_count, dtype=jnp.int32)[None, :]
    own_select = (own_picks[:, None] == patch_ids).astype(jnp.bfloat16)
    other_select = (other_picks[:, None] == patch_ids).astype(jnp.bfloat16)
    received_heads = swap(
        jnp.dot(other_select, attended, preferred_element_type=jnp.float32).astype(jnp.bfloat16)
    )
    own_heads = jnp.dot(own_select, attended, preferred_element_type=jnp.float32).astype(
        jnp.bfloat16
    )
    own_rows = jnp.concatenate([own_heads, received_heads], 1)
    full_out = jnp.concatenate([vision_out, vision_out_other], 0)
    kept = (
        jnp.dot(own_select, patches, preferred_element_type=jnp.float32)
        + jnp.dot(own_rows, full_out, preferred_element_type=jnp.float32)
    ).astype(jnp.bfloat16)
    merge_terms = jnp.dot(
        kept.reshape(merged_count, 2 * D),
        projector.reshape(2 * D, D),
        preferred_element_type=jnp.float32,
    )
    image_rows = (merge_terms + swap(merge_terms)).astype(jnp.bfloat16)

    per_peer = merged_count // seq_count
    run_starts = dest_positions.reshape(seq_count, merged_count)[:, 0]
    own_start = run_starts[seq_index]
    received = lax.all_to_all(
        jnp.transpose(
            jnp.roll(image_rows.reshape(per_peer, seq_count, D), own_start, axis=1), (1, 0, 2)
        ),
        "seq",
        split_axis=0,
        concat_axis=0,
        tiled=True,
    )
    slot_base = jnp.arange(per_peer, dtype=jnp.int32)[:, None] * seq_count
    landing = (
        run_starts[None, :] + slot_base + (seq_index - run_starts[None, :]) % seq_count
    ) // seq_count
    text_rows = text_embeds.shape[0]
    prompt = text_embeds.reshape(text_rows, D).at[landing.T.reshape(-1)].set(received.reshape(-1, D))
    text_normed = root_norm(prompt).astype(jnp.bfloat16)
    head_queries = root_norm(
        jnp.einsum(
            "td,dhe->hte",
            text_normed,
            decoder_q.reshape(D, local_heads, HEAD),
            preferred_element_type=jnp.float32,
        )
    ).astype(jnp.bfloat16)
    paired = jnp.dot(
        text_normed, decoder_kv.reshape(D, -1), preferred_element_type=jnp.float32
    ).reshape(text_rows, 2, HEAD)
    key_rows = root_norm(paired[:, 0]).astype(jnp.bfloat16)
    value_rows = paired[:, 1].astype(jnp.bfloat16)

    shared = jnp.stack([key_rows, value_rows], 0)[None]
    piece = lax.all_gather(shared, "seq", axis=0, tiled=True)
    rows = 64
    doc_starts = jnp.sum(
        (segment_ids[None] < jnp.arange(4, dtype=jnp.int32)[:, None, None]).astype(jnp.int32),
        (1, 2),
    )
    info = jnp.concatenate(
        [doc_starts, jnp.full((1,), seq_index, jnp.int32), jnp.zeros((3,), jnp.int32)]
    )
    decoder_out_full, head_queries = lax.optimization_barrier(
        (in_head_order(first, decoder_out, decoder_out_other, 0), head_queries)
    )
    head_major = text_attention(info, head_queries, piece, rows, scale)
    attended_text = jnp.transpose(head_major, (1, 0, 2)).reshape(text_rows, -1)
    all_heads = in_head_order(first, attended_text, swap(attended_text), 1)
    output_terms = jnp.dot(all_heads, decoder_out_full, preferred_element_type=jnp.float32)
    decoded = (prompt.astype(jnp.float32) + output_terms).astype(jnp.bfloat16)
    return decoded.reshape(text_rows, 1, D)


def solution(mesh):
    placed = (
        P("seq", None),
        P("seq", None),
        P("seq"),
        P(),
        P(None, "seq", None),
        P(),
        P(None, None, "section"),
        P("section", None),
        P("section", None, None),
        P(None, "section"),
        P(None, None, "section"),
        P("section", None),
    )
    return jax.shard_map(
        body, mesh=mesh, in_specs=placed, out_specs=P(None, "seq", None), check_vma=False
    )
```

```python
import math

import jax
import jax.numpy as jnp
from jax import lax
from jax.sharding import PartitionSpec as P
from jax.experimental import pallas as pl
from jax.experimental.pallas import tpu as pltpu
import functools

D = 1408
HEAD = 88


def layer_norm(values):
    values = values.astype(jnp.float32)
    centred = values - jnp.mean(values, -1, keepdims=True)
    return centred * lax.rsqrt(jnp.mean(centred * centred, -1, keepdims=True) + 1e-06)


def root_norm(values):
    values = values.astype(jnp.float32)
    return values * lax.rsqrt(jnp.mean(values * values, -1, keepdims=True) + 1e-06)


def merge_rows(grid, offsets, count):
    heights = grid[:, 0]
    widths = grid[:, 1]
    group_start = offsets // 4
    group_count = heights * widths // 4
    merged_ids = jnp.arange(count, dtype=jnp.int32)
    inside = (
        (merged_ids[:, None] >= group_start[None, :])
        & (merged_ids[:, None] < (group_start + group_count)[None, :])
    ).astype(jnp.int32)
    first_group = jnp.sum(inside * group_start[None, :], 1)
    first_patch = jnp.sum(inside * offsets[None, :], 1)
    row_width = jnp.sum(inside * widths[None, :], 1)
    within = merged_ids - first_group
    groups_across = row_width // 2
    group_row = within // groups_across
    group_col = within % groups_across
    corner = first_patch + 2 * group_row * row_width + 2 * group_col
    return jnp.stack([corner, corner + 1, corner + row_width, corner + row_width + 1], 1)


def _segment_start(info_ref, places):
    start = jnp.zeros_like(places) + info_ref[0]
    for doc in range(1, 4):
        bound = info_ref[doc]
        start = jnp.where(places >= bound, bound, start)
    return start


def _first_block(info_ref, qb, span):
    return _segment_start(info_ref, qb * span + info_ref[4]) // span


def _text_kernel(query_block_ref, key_block_ref, info_ref, q_ref, kv_ref, o_ref, acc_ref, ext_ref, *, scale):
    step = pl.program_id(0)
    qb = query_block_ref[step]
    kb = key_block_ref[step]
    heads, rows, head = q_ref.shape
    shards = kv_ref.shape[0]
    span = rows * shards
    own = info_ref[4]
    last_query = qb * span + own + (rows - 1) * shards
    active = kb >= _first_block(info_ref, qb, span)
    unmasked = (kb < qb) & (kb * span >= _segment_start(info_ref, last_query))

    @pl.when(step == 0)
    def _():
        lane = lax.broadcasted_iota(jnp.int32, ext_ref.shape, 1)
        ext_ref[...] = jnp.where(lane == head, 1.0, 0.0).astype(ext_ref.dtype)

    @pl.when(kb == 0)
    def _():
        acc_ref[...] = jnp.zeros_like(acc_ref)

    def accumulate(masked):
        q = q_ref[...].reshape(heads * rows, head)
        k = kv_ref[:, 0].reshape(span, head)
        ext_ref[:, :head] = kv_ref[:, 1].reshape(span, head)
        s = lax.dot_general(q, k, (((1,), (1,)), ((), ())), preferred_element_type=jnp.float32)
        w = jnp.exp(s * scale)
        if masked:
            row = lax.broadcasted_iota(jnp.int32, (heads * rows, 1), 0) & (rows - 1)
            query_places = (qb * rows + row) * shards + own
            lane = lax.broadcasted_iota(jnp.int32, (1, span), 1)
            key_places = (kb * rows + (lane & (rows - 1))) * shards + lax.shift_right_logical(
                lane, rows.bit_length() - 1
            )
            allowed = (key_places <= query_places) & (
                key_places >= _segment_start(info_ref, query_places)
            )
            w = jnp.where(allowed, w, 0.0)
        acc_ref[...] += jnp.dot(
            w.astype(jnp.bfloat16), ext_ref[...], preferred_element_type=jnp.float32
        )

    @pl.when(active & unmasked)
    def _():
        accumulate(False)

    @pl.when(active & jnp.logical_not(unmasked))
    def _():
        accumulate(True)

    @pl.when(kb == qb)
    def _():
        acc = acc_ref[...]
        o_ref[...] = (acc[:, :head] / acc[:, head : head + 1]).astype(o_ref.dtype).reshape(
            o_ref.shape
        )


def text_attention(info, q, kv, rows, scale):
    heads, text_rows, head = q.shape
    shards = kv.shape[0]
    blocks = text_rows // rows
    span = rows * shards
    pairs = [(i, j) for i in range(blocks) for j in range(i + 1)]
    query_block = jnp.array([i for i, _ in pairs], jnp.int32)
    key_block = jnp.array([j for _, j in pairs], jnp.int32)

    def q_block(t, qb_ref, kb_ref, info_ref):
        return (0, qb_ref[t], 0)

    def kv_block(t, qb_ref, kb_ref, info_ref):
        qb = qb_ref[t]
        return (0, 0, jnp.maximum(kb_ref[t], _first_block(info_ref, qb, span)), 0)

    return pl.pallas_call(
        functools.partial(_text_kernel, scale=scale),
        grid_spec=pltpu.PrefetchScalarGridSpec(
            num_scalar_prefetch=3,
            grid=(len(pairs),),
            in_specs=[
                pl.BlockSpec((heads, rows, head), q_block),
                pl.BlockSpec((shards, 2, rows, head), kv_block),
            ],
            out_specs=pl.BlockSpec((heads, rows, head), q_block),
            scratch_shapes=[
                pltpu.VMEM((heads * rows, 128), jnp.float32),
                pltpu.VMEM((span, 128), jnp.bfloat16),
            ],
        ),
        out_shape=jax.ShapeDtypeStruct((heads, text_rows, head), jnp.bfloat16),
        compiler_params=pltpu.CompilerParams(dimension_semantics=("arbitrary",)),
    )(query_block, key_block, info, q, kv)


def swap(values):
    return lax.ppermute(values, "section", [(0, 1), (1, 0)])


def in_head_order(first, own, other, axis):
    return jnp.where(
        first, jnp.concatenate([own, other], axis), jnp.concatenate([other, own], axis)
    )


def body(
    patches,
    image_grid,
    image_offsets,
    dest_positions,
    text_embeds,
    segment_ids,
    vision_qkv,
    vision_out,
    projector,
    decoder_q,
    decoder_kv,
    decoder_out,
):
    section_index = lax.axis_index("section")
    seq_index = lax.axis_index("seq")
    seq_count = lax.axis_size("seq")
    first = section_index == 0
    scale = 3.0 / math.sqrt(HEAD)
    patch_count = patches.shape[0]
    local_heads = vision_out.shape[0] // HEAD
    merged_count = patch_count // 4

    vision_out_other = swap(vision_out)
    decoder_out_other = swap(decoder_out)

    normed = layer_norm(patches).astype(jnp.bfloat16)
    mixed = jnp.dot(normed, vision_qkv.reshape(D, -1), preferred_element_type=jnp.float32).reshape(
        patch_count, 3, local_heads, HEAD
    )
    queries = root_norm(mixed[:, 0]).astype(jnp.bfloat16)
    keys = root_norm(mixed[:, 1]).astype(jnp.bfloat16)
    values = mixed[:, 2].astype(jnp.bfloat16)
    offsets = image_offsets - seq_index * patch_count
    image_of = jnp.sum(
        (jnp.arange(patch_count, dtype=jnp.int32)[:, None] >= offsets[None, :]).astype(jnp.int32), 1
    )
    scores = jnp.einsum("qhd,khd->hqk", queries, keys, preferred_element_type=jnp.float32) * scale
    same = (image_of[:, None] == image_of[None, :])[None]
    weights = jnp.where(same, jnp.exp(scores), jnp.zeros_like(scores))
    totals = jnp.sum(weights, -1)
    mixed_values = jnp.einsum(
        "hqk,khd->qhd", weights.astype(jnp.bfloat16), values, preferred_element_type=jnp.float32
    )
    attended = (
        (mixed_values / jnp.transpose(totals)[:, :, None])
        .astype(jnp.bfloat16)
        .reshape(patch_count, local_heads * HEAD)
    )
    per_peer = merged_count // seq_count
    run_starts = dest_positions.reshape(seq_count, merged_count)[:, 0]
    own_start = run_starts[seq_index]
    send_order = (
        jnp.arange(per_peer, dtype=jnp.int32)[None, :] * seq_count
        + (jnp.arange(seq_count, dtype=jnp.int32)[:, None] - own_start) % seq_count
    ).reshape(-1)
    picks = merge_rows(image_grid, offsets, merged_count)[send_order]
    own_picks = lax.dynamic_slice_in_dim(picks, 2 * section_index, 2, 1).reshape(-1)
    other_picks = lax.dynamic_slice_in_dim(picks, 2 - 2 * section_index, 2, 1).reshape(-1)
    patch_ids = jnp.arange(patch_count, dtype=jnp.int32)[None, :]
    own_select = (own_picks[:, None] == patch_ids).astype(jnp.bfloat16)
    other_select = (other_picks[:, None] == patch_ids).astype(jnp.bfloat16)
    received_heads = swap(
        jnp.dot(other_select, attended, preferred_element_type=jnp.float32).astype(jnp.bfloat16)
    )
    own_heads = jnp.dot(own_select, attended, preferred_element_type=jnp.float32).astype(
        jnp.bfloat16
    )
    own_rows = jnp.concatenate([own_heads, received_heads], 1)
    full_out = jnp.concatenate([vision_out, vision_out_other], 0)
    kept = (
        jnp.dot(own_select, patches, preferred_element_type=jnp.float32)
        + jnp.dot(own_rows, full_out, preferred_element_type=jnp.float32)
    ).astype(jnp.bfloat16)
    halves = []
    for half in jnp.split(kept.reshape(merged_count, 2 * D), 2):
        merge_terms = jnp.dot(
            half, projector.reshape(2 * D, D), preferred_element_type=jnp.float32
        )
        halves.append((merge_terms + swap(merge_terms)).astype(jnp.bfloat16))
    image_rows = jnp.concatenate(halves)

    received = lax.all_to_all(
        image_rows.reshape(seq_count, per_peer, D),
        "seq",
        split_axis=0,
        concat_axis=0,
        tiled=True,
    )
    slot_base = jnp.arange(per_peer, dtype=jnp.int32)[:, None] * seq_count
    landing = (
        run_starts[None, :] + slot_base + (seq_index - run_starts[None, :]) % seq_count
    ) // seq_count
    text_rows = text_embeds.shape[0]
    prompt = text_embeds.reshape(text_rows, D).at[landing.T.reshape(-1)].set(received.reshape(-1, D))
    text_normed = root_norm(prompt).astype(jnp.bfloat16)
    head_queries = root_norm(
        jnp.einsum(
            "td,dhe->hte",
            text_normed,
            decoder_q.reshape(D, local_heads, HEAD),
            preferred_element_type=jnp.float32,
        )
    ).astype(jnp.bfloat16)
    paired = jnp.dot(
        text_normed, decoder_kv.reshape(D, -1), preferred_element_type=jnp.float32
    ).reshape(text_rows, 2, HEAD)
    key_rows = root_norm(paired[:, 0]).astype(jnp.bfloat16)
    value_rows = paired[:, 1].astype(jnp.bfloat16)

    shared = jnp.stack([key_rows, value_rows], 0)[None]
    piece = lax.all_gather(shared, "seq", axis=0, tiled=True)
    rows = 64
    doc_starts = jnp.sum(
        (segment_ids[None] < jnp.arange(4, dtype=jnp.int32)[:, None, None]).astype(jnp.int32),
        (1, 2),
    )
    info = jnp.concatenate(
        [doc_starts, jnp.full((1,), seq_index, jnp.int32), jnp.zeros((3,), jnp.int32)]
    )
    decoder_out_full, head_queries = lax.optimization_barrier(
        (in_head_order(first, decoder_out, decoder_out_other, 0), head_queries)
    )
    head_major = text_attention(info, head_queries, piece, rows, scale)
    attended_text = jnp.transpose(head_major, (1, 0, 2)).reshape(text_rows, -1)
    all_heads = in_head_order(first, attended_text, swap(attended_text), 1)
    output_terms = jnp.dot(all_heads, decoder_out_full, preferred_element_type=jnp.float32)
    decoded = (prompt.astype(jnp.float32) + output_terms).astype(jnp.bfloat16)
    return decoded.reshape(text_rows, 1, D)


def solution(mesh):
    placed = (
        P("seq", None),
        P("seq", None),
        P("seq"),
        P(),
        P(None, "seq", None),
        P(),
        P(None, None, "section"),
        P("section", None),
        P("section", None, None),
        P(None, "section"),
        P(None, None, "section"),
        P("section", None),
    )
    return jax.shard_map(
        body, mesh=mesh, in_specs=placed, out_specs=P(None, "seq", None), check_vma=False
    )
```

```python
import math

import jax
import jax.numpy as jnp
from jax import lax
from jax.sharding import PartitionSpec as P
from jax.experimental import pallas as pl
from jax.experimental.pallas import tpu as pltpu
import functools

D = 1408
HEAD = 88


def layer_norm(values):
    values = values.astype(jnp.float32)
    centred = values - jnp.mean(values, -1, keepdims=True)
    return centred * lax.rsqrt(jnp.mean(centred * centred, -1, keepdims=True) + 1e-06)


def root_norm(values):
    values = values.astype(jnp.float32)
    return values * lax.rsqrt(jnp.mean(values * values, -1, keepdims=True) + 1e-06)


def merge_rows(grid, offsets, count):
    heights = grid[:, 0]
    widths = grid[:, 1]
    group_start = offsets // 4
    group_count = heights * widths // 4
    merged_ids = jnp.arange(count, dtype=jnp.int32)
    inside = (
        (merged_ids[:, None] >= group_start[None, :])
        & (merged_ids[:, None] < (group_start + group_count)[None, :])
    ).astype(jnp.int32)
    first_group = jnp.sum(inside * group_start[None, :], 1)
    first_patch = jnp.sum(inside * offsets[None, :], 1)
    row_width = jnp.sum(inside * widths[None, :], 1)
    within = merged_ids - first_group
    groups_across = row_width // 2
    group_row = within // groups_across
    group_col = within % groups_across
    corner = first_patch + 2 * group_row * row_width + 2 * group_col
    return jnp.stack([corner, corner + 1, corner + row_width, corner + row_width + 1], 1)


def _segment_start(info_ref, places):
    start = jnp.zeros_like(places) + info_ref[0]
    for doc in range(1, 4):
        bound = info_ref[doc]
        start = jnp.where(places >= bound, bound, start)
    return start


def _first_block(info_ref, qb, span):
    return _segment_start(info_ref, qb * span + info_ref[4]) // span


def _text_kernel(query_block_ref, key_block_ref, info_ref, q_ref, kv_ref, o_ref, acc_ref, ext_ref, *, scale):
    step = pl.program_id(0)
    qb = query_block_ref[step]
    kb = key_block_ref[step]
    heads, rows, head = q_ref.shape
    shards = kv_ref.shape[0]
    span = rows * shards
    own = info_ref[4]
    last_query = qb * span + own + (rows - 1) * shards
    active = kb >= _first_block(info_ref, qb, span)
    unmasked = (kb < qb) & (kb * span >= _segment_start(info_ref, last_query))

    @pl.when(step == 0)
    def _():
        lane = lax.broadcasted_iota(jnp.int32, ext_ref.shape, 1)
        ext_ref[...] = jnp.where(lane == head, 1.0, 0.0).astype(ext_ref.dtype)

    @pl.when(kb == 0)
    def _():
        acc_ref[...] = jnp.zeros_like(acc_ref)

    def accumulate(masked):
        q = q_ref[...].reshape(heads * rows, head)
        k = kv_ref[:, 0].reshape(span, head)
        ext_ref[:, :head] = kv_ref[:, 1].reshape(span, head)
        s = lax.dot_general(q, k, (((1,), (1,)), ((), ())), preferred_element_type=jnp.float32)
        w = jnp.exp(s * scale)
        if masked:
            row = lax.broadcasted_iota(jnp.int32, (heads * rows, 1), 0) & (rows - 1)
            query_places = (qb * rows + row) * shards + own
            lane = lax.broadcasted_iota(jnp.int32, (1, span), 1)
            key_places = (kb * rows + (lane & (rows - 1))) * shards + lax.shift_right_logical(
                lane, rows.bit_length() - 1
            )
            allowed = (key_places <= query_places) & (
                key_places >= _segment_start(info_ref, query_places)
            )
            w = jnp.where(allowed, w, 0.0)
        acc_ref[...] += jnp.dot(
            w.astype(jnp.bfloat16), ext_ref[...], preferred_element_type=jnp.float32
        )

    @pl.when(active & unmasked)
    def _():
        accumulate(False)

    @pl.when(active & jnp.logical_not(unmasked))
    def _():
        accumulate(True)

    @pl.when(kb == qb)
    def _():
        acc = acc_ref[...]
        o_ref[...] = (acc[:, :head] / acc[:, head : head + 1]).astype(o_ref.dtype).reshape(
            o_ref.shape
        )


def text_attention(info, q, kv, rows, scale):
    heads, text_rows, head = q.shape
    shards = kv.shape[0]
    blocks = text_rows // rows
    span = rows * shards
    pairs = [(i, j) for i in range(blocks) for j in range(i + 1)]
    query_block = jnp.array([i for i, _ in pairs], jnp.int32)
    key_block = jnp.array([j for _, j in pairs], jnp.int32)

    def q_block(t, qb_ref, kb_ref, info_ref):
        return (0, qb_ref[t], 0)

    def kv_block(t, qb_ref, kb_ref, info_ref):
        qb = qb_ref[t]
        return (0, 0, jnp.maximum(kb_ref[t], _first_block(info_ref, qb, span)), 0)

    return pl.pallas_call(
        functools.partial(_text_kernel, scale=scale),
        grid_spec=pltpu.PrefetchScalarGridSpec(
            num_scalar_prefetch=3,
            grid=(len(pairs),),
            in_specs=[
                pl.BlockSpec((heads, rows, head), q_block),
                pl.BlockSpec((shards, 2, rows, head), kv_block),
            ],
            out_specs=pl.BlockSpec((heads, rows, head), q_block),
            scratch_shapes=[
                pltpu.VMEM((heads * rows, 128), jnp.float32),
                pltpu.VMEM((span, 128), jnp.bfloat16),
            ],
        ),
        out_shape=jax.ShapeDtypeStruct((heads, text_rows, head), jnp.bfloat16),
        compiler_params=pltpu.CompilerParams(dimension_semantics=("arbitrary",)),
    )(query_block, key_block, info, q, kv)


def swap(values):
    return lax.ppermute(values, "section", [(0, 1), (1, 0)])


def in_head_order(first, own, other, axis):
    return jnp.where(
        first, jnp.concatenate([own, other], axis), jnp.concatenate([other, own], axis)
    )


def body(
    patches,
    image_grid,
    image_offsets,
    dest_positions,
    text_embeds,
    segment_ids,
    vision_qkv,
    vision_out,
    projector,
    decoder_q,
    decoder_kv,
    decoder_out,
):
    section_index = lax.axis_index("section")
    seq_index = lax.axis_index("seq")
    seq_count = lax.axis_size("seq")
    first = section_index == 0
    scale = 3.0 / math.sqrt(HEAD)
    patch_count = patches.shape[0]
    local_heads = vision_out.shape[0] // HEAD
    merged_count = patch_count // 4

    vision_out_other = swap(vision_out)
    decoder_out_other = swap(decoder_out)

    normed = layer_norm(patches).astype(jnp.bfloat16)
    mixed = jnp.dot(normed, vision_qkv.reshape(D, -1), preferred_element_type=jnp.float32).reshape(
        patch_count, 3, local_heads, HEAD
    )
    queries = root_norm(mixed[:, 0]).astype(jnp.bfloat16)
    keys = root_norm(mixed[:, 1]).astype(jnp.bfloat16)
    values = mixed[:, 2].astype(jnp.bfloat16)
    offsets = image_offsets - seq_index * patch_count
    image_of = jnp.sum(
        (jnp.arange(patch_count, dtype=jnp.int32)[:, None] >= offsets[None, :]).astype(jnp.int32), 1
    )
    scores = jnp.einsum("qhd,khd->hqk", queries, keys, preferred_element_type=jnp.float32) * scale
    same = (image_of[:, None] == image_of[None, :])[None]
    weights = jnp.where(same, jnp.exp(scores), jnp.zeros_like(scores))
    totals = jnp.sum(weights, -1)
    mixed_values = jnp.einsum(
        "hqk,khd->qhd", weights.astype(jnp.bfloat16), values, preferred_element_type=jnp.float32
    )
    attended = (
        (mixed_values / jnp.transpose(totals)[:, :, None])
        .astype(jnp.bfloat16)
        .reshape(patch_count, local_heads * HEAD)
    )
    picks = merge_rows(image_grid, offsets, merged_count)
    own_picks = lax.dynamic_slice_in_dim(picks, 2 * section_index, 2, 1).reshape(-1)
    other_picks = lax.dynamic_slice_in_dim(picks, 2 - 2 * section_index, 2, 1).reshape(-1)
    patch_ids = jnp.arange(patch_count, dtype=jnp.int32)[None, :]
    own_select = (own_picks[:, None] == patch_ids).astype(jnp.bfloat16)
    other_select = (other_picks[:, None] == patch_ids).astype(jnp.bfloat16)
    received_heads = swap(
        jnp.dot(other_select, attended, preferred_element_type=jnp.float32).astype(jnp.bfloat16)
    )
    own_heads = jnp.dot(own_select, attended, preferred_element_type=jnp.float32).astype(
        jnp.bfloat16
    )
    own_rows = jnp.concatenate([own_heads, received_heads], 1)
    full_out = jnp.concatenate([vision_out, vision_out_other], 0)
    kept = (
        jnp.dot(own_select, patches, preferred_element_type=jnp.float32)
        + jnp.dot(own_rows, full_out, preferred_element_type=jnp.float32)
    ).astype(jnp.bfloat16)
    merge_terms = jnp.dot(
        kept.reshape(merged_count, 2 * D),
        projector.reshape(2 * D, D),
        preferred_element_type=jnp.float32,
    )
    image_rows = (merge_terms + swap(merge_terms)).astype(jnp.bfloat16)

    per_peer = merged_count // seq_count
    run_starts = dest_positions.reshape(seq_count, merged_count)[:, 0]
    own_start = run_starts[seq_index]
    received = lax.all_to_all(
        jnp.transpose(
            jnp.roll(image_rows.reshape(per_peer, seq_count, D), own_start, axis=1), (1, 0, 2)
        ),
        "seq",
        split_axis=0,
        concat_axis=0,
        tiled=True,
    )
    slot_base = jnp.arange(per_peer, dtype=jnp.int32)[:, None] * seq_count
    landing = (
        run_starts[None, :] + slot_base + (seq_index - run_starts[None, :]) % seq_count
    ) // seq_count
    text_rows = text_embeds.shape[0]
    prompt = text_embeds.reshape(text_rows, D).at[landing.T.reshape(-1)].set(received.reshape(-1, D))
    text_normed = root_norm(prompt).astype(jnp.bfloat16)
    head_queries = root_norm(
        jnp.einsum(
            "td,dhe->hte",
            text_normed,
            decoder_q.reshape(D, local_heads, HEAD),
            preferred_element_type=jnp.float32,
        )
    ).astype(jnp.bfloat16)
    paired = jnp.dot(
        text_normed, decoder_kv.reshape(D, -1), preferred_element_type=jnp.float32
    ).reshape(text_rows, 2, HEAD)
    key_rows = root_norm(paired[:, 0]).astype(jnp.bfloat16)
    value_rows = paired[:, 1].astype(jnp.bfloat16)

    shared = jnp.stack([key_rows, value_rows], 0)[None]
    piece = lax.all_gather(shared, "seq", axis=0, tiled=True)
    rows = 64
    doc_starts = jnp.sum(
        (segment_ids[None] < jnp.arange(4, dtype=jnp.int32)[:, None, None]).astype(jnp.int32),
        (1, 2),
    )
    info = jnp.concatenate(
        [doc_starts, jnp.full((1,), seq_index, jnp.int32), jnp.zeros((3,), jnp.int32)]
    )
    decoder_out_full, head_queries = lax.optimization_barrier(
        (in_head_order(first, decoder_out, decoder_out_other, 0), head_queries)
    )
    head_major = text_attention(info, head_queries, piece, rows, scale)
    all_heads = in_head_order(first, head_major, swap(head_major), 0)
    output_terms = jnp.einsum(
        "hte,hed->td",
        all_heads,
        decoder_out_full.reshape(2 * local_heads, HEAD, D),
        preferred_element_type=jnp.float32,
    )
    decoded = (prompt.astype(jnp.float32) + output_terms).astype(jnp.bfloat16)
    return decoded.reshape(text_rows, 1, D)


def solution(mesh):
    placed = (
        P("seq", None),
        P("seq", None),
        P("seq"),
        P(),
        P(None, "seq", None),
        P(),
        P(None, None, "section"),
        P("section", None),
        P("section", None, None),
        P(None, "section"),
        P(None, None, "section"),
        P("section", None),
    )
    return jax.shard_map(
        body, mesh=mesh, in_specs=placed, out_specs=P(None, "seq", None), check_vma=False
    )
```

```python
import math

import jax
import jax.numpy as jnp
from jax import lax
from jax.sharding import PartitionSpec as P
from jax.experimental import pallas as pl
from jax.experimental.pallas import tpu as pltpu
import functools

D = 1408
HEAD = 88


def layer_norm(values):
    values = values.astype(jnp.float32)
    centred = values - jnp.mean(values, -1, keepdims=True)
    return centred * lax.rsqrt(jnp.mean(centred * centred, -1, keepdims=True) + 1e-06)


def root_norm(values):
    values = values.astype(jnp.float32)
    return values * lax.rsqrt(jnp.mean(values * values, -1, keepdims=True) + 1e-06)


def merge_rows(grid, offsets, count):
    heights = grid[:, 0]
    widths = grid[:, 1]
    group_start = offsets // 4
    group_count = heights * widths // 4
    merged_ids = jnp.arange(count, dtype=jnp.int32)
    inside = (
        (merged_ids[:, None] >= group_start[None, :])
        & (merged_ids[:, None] < (group_start + group_count)[None, :])
    ).astype(jnp.int32)
    first_group = jnp.sum(inside * group_start[None, :], 1)
    first_patch = jnp.sum(inside * offsets[None, :], 1)
    row_width = jnp.sum(inside * widths[None, :], 1)
    within = merged_ids - first_group
    groups_across = row_width // 2
    group_row = within // groups_across
    group_col = within % groups_across
    corner = first_patch + 2 * group_row * row_width + 2 * group_col
    return jnp.stack([corner, corner + 1, corner + row_width, corner + row_width + 1], 1)


def _segment_start(info_ref, places):
    start = jnp.zeros_like(places) + info_ref[0]
    for doc in range(1, 4):
        bound = info_ref[doc]
        start = jnp.where(places >= bound, bound, start)
    return start


def _first_block(info_ref, qb, span):
    return _segment_start(info_ref, qb * span + info_ref[4]) // span


def _text_kernel(query_block_ref, key_block_ref, info_ref, q_ref, kv_ref, o_ref, acc_ref, ext_ref, *, scale):
    step = pl.program_id(0)
    qb = query_block_ref[step]
    kb = key_block_ref[step]
    heads, rows, head = q_ref.shape
    shards = kv_ref.shape[0]
    span = rows * shards
    own = info_ref[4]
    last_query = qb * span + own + (rows - 1) * shards
    active = kb >= _first_block(info_ref, qb, span)
    unmasked = (kb < qb) & (kb * span >= _segment_start(info_ref, last_query))

    @pl.when(step == 0)
    def _():
        lane = lax.broadcasted_iota(jnp.int32, ext_ref.shape, 1)
        ext_ref[...] = jnp.where(lane == head, 1.0, 0.0).astype(ext_ref.dtype)

    @pl.when(kb == 0)
    def _():
        acc_ref[...] = jnp.zeros_like(acc_ref)

    def accumulate(masked):
        q = q_ref[...].reshape(heads * rows, head)
        k = kv_ref[:, 0].reshape(span, head)
        ext_ref[:, :head] = kv_ref[:, 1].reshape(span, head)
        s = lax.dot_general(q, k, (((1,), (1,)), ((), ())), preferred_element_type=jnp.float32)
        w = jnp.exp(s * scale)
        if masked:
            row = lax.broadcasted_iota(jnp.int32, (heads * rows, 1), 0) & (rows - 1)
            query_places = (qb * rows + row) * shards + own
            lane = lax.broadcasted_iota(jnp.int32, (1, span), 1)
            key_places = (kb * rows + (lane & (rows - 1))) * shards + lax.shift_right_logical(
                lane, rows.bit_length() - 1
            )
            allowed = (key_places <= query_places) & (
                key_places >= _segment_start(info_ref, query_places)
            )
            w = jnp.where(allowed, w, 0.0)
        acc_ref[...] += jnp.dot(
            w.astype(jnp.bfloat16), ext_ref[...], preferred_element_type=jnp.float32
        )

    @pl.when(active & unmasked)
    def _():
        accumulate(False)

    @pl.when(active & jnp.logical_not(unmasked))
    def _():
        accumulate(True)

    @pl.when(kb == qb)
    def _():
        acc = acc_ref[...]
        o_ref[...] = (acc[:, :head] / acc[:, head : head + 1]).astype(o_ref.dtype).reshape(
            o_ref.shape
        )


def text_attention(info, q, kv, rows, scale):
    heads, text_rows, head = q.shape
    shards = kv.shape[0]
    blocks = text_rows // rows
    span = rows * shards
    pairs = [(i, j) for i in range(blocks) for j in range(i + 1)]
    query_block = jnp.array([i for i, _ in pairs], jnp.int32)
    key_block = jnp.array([j for _, j in pairs], jnp.int32)

    def q_block(t, qb_ref, kb_ref, info_ref):
        return (0, qb_ref[t], 0)

    def kv_block(t, qb_ref, kb_ref, info_ref):
        qb = qb_ref[t]
        return (0, 0, jnp.maximum(kb_ref[t], _first_block(info_ref, qb, span)), 0)

    return pl.pallas_call(
        functools.partial(_text_kernel, scale=scale),
        grid_spec=pltpu.PrefetchScalarGridSpec(
            num_scalar_prefetch=3,
            grid=(len(pairs),),
            in_specs=[
                pl.BlockSpec((heads, rows, head), q_block),
                pl.BlockSpec((shards, 2, rows, head), kv_block),
            ],
            out_specs=pl.BlockSpec((heads, rows, head), q_block),
            scratch_shapes=[
                pltpu.VMEM((heads * rows, 128), jnp.float32),
                pltpu.VMEM((span, 128), jnp.bfloat16),
            ],
        ),
        out_shape=jax.ShapeDtypeStruct((heads, text_rows, head), jnp.bfloat16),
        compiler_params=pltpu.CompilerParams(dimension_semantics=("arbitrary",)),
    )(query_block, key_block, info, q, kv)


def swap(values):
    return lax.ppermute(values, "section", [(0, 1), (1, 0)])


def in_head_order(first, own, other, axis):
    return jnp.where(
        first, jnp.concatenate([own, other], axis), jnp.concatenate([other, own], axis)
    )


def body(
    patches,
    image_grid,
    image_offsets,
    dest_positions,
    text_embeds,
    segment_ids,
    vision_qkv,
    vision_out,
    projector,
    decoder_q,
    decoder_kv,
    decoder_out,
):
    section_index = lax.axis_index("section")
    seq_index = lax.axis_index("seq")
    seq_count = lax.axis_size("seq")
    first = section_index == 0
    scale = 3.0 / math.sqrt(HEAD)
    patch_count = patches.shape[0]
    local_heads = vision_out.shape[0] // HEAD
    merged_count = patch_count // 4

    vision_out_other = swap(vision_out)
    decoder_out_other = swap(decoder_out)

    normed = layer_norm(patches).astype(jnp.bfloat16)
    mixed = jnp.dot(normed, vision_qkv.reshape(D, -1), preferred_element_type=jnp.float32).reshape(
        patch_count, 3, local_heads, HEAD
    )
    queries = root_norm(mixed[:, 0]).astype(jnp.bfloat16)
    keys = root_norm(mixed[:, 1]).astype(jnp.bfloat16)
    values = mixed[:, 2].astype(jnp.bfloat16)
    offsets = image_offsets - seq_index * patch_count
    image_of = jnp.sum(
        (jnp.arange(patch_count, dtype=jnp.int32)[:, None] >= offsets[None, :]).astype(jnp.int32), 1
    )
    scores = jnp.einsum("qhd,khd->hqk", queries, keys, preferred_element_type=jnp.float32) * scale
    same = (image_of[:, None] == image_of[None, :])[None]
    weights = jnp.where(same, jnp.exp(scores), jnp.zeros_like(scores))
    totals = jnp.sum(weights, -1)
    mixed_values = jnp.einsum(
        "hqk,khd->qhd", weights.astype(jnp.bfloat16), values, preferred_element_type=jnp.float32
    )
    attended = (
        (mixed_values / jnp.transpose(totals)[:, :, None])
        .astype(jnp.bfloat16)
        .reshape(patch_count, local_heads * HEAD)
    )
    picks = merge_rows(image_grid, offsets, merged_count)
    own_picks = lax.dynamic_slice_in_dim(picks, 2 * section_index, 2, 1).reshape(-1)
    other_picks = lax.dynamic_slice_in_dim(picks, 2 - 2 * section_index, 2, 1).reshape(-1)
    patch_ids = jnp.arange(patch_count, dtype=jnp.int32)[None, :]
    own_select = (own_picks[:, None] == patch_ids).astype(jnp.bfloat16)
    other_select = (other_picks[:, None] == patch_ids).astype(jnp.bfloat16)
    received_heads = swap(
        jnp.dot(other_select, attended, preferred_element_type=jnp.float32).astype(jnp.bfloat16)
    )
    own_heads = jnp.dot(own_select, attended, preferred_element_type=jnp.float32).astype(
        jnp.bfloat16
    )
    own_rows = jnp.concatenate([own_heads, received_heads], 1)
    full_out = jnp.concatenate([vision_out, vision_out_other], 0)
    kept = (
        jnp.dot(own_select, patches, preferred_element_type=jnp.float32)
        + jnp.dot(own_rows, full_out, preferred_element_type=jnp.float32)
    ).astype(jnp.bfloat16)
    merge_terms = jnp.dot(
        kept.reshape(merged_count, 2 * D),
        projector.reshape(2 * D, D),
        preferred_element_type=jnp.float32,
    )
    image_rows = (merge_terms + swap(merge_terms)).astype(jnp.bfloat16)

    per_peer = merged_count // seq_count
    run_starts = dest_positions.reshape(seq_count, merged_count)[:, 0]
    own_start = run_starts[seq_index]
    def key_value(rows_in):
        normed_rows = root_norm(rows_in).astype(jnp.bfloat16)
        paired = jnp.dot(
            normed_rows, decoder_kv.reshape(D, -1), preferred_element_type=jnp.float32
        ).reshape(rows_in.shape[0], 2, HEAD)
        return (root_norm(paired[:, 0]).astype(jnp.bfloat16), paired[:, 1].astype(jnp.bfloat16))

    text_kv = key_value(text_embeds.reshape(text_embeds.shape[0], D))
    received = lax.all_to_all(
        jnp.transpose(
            jnp.roll(image_rows.reshape(per_peer, seq_count, D), own_start, axis=1), (1, 0, 2)
        ),
        "seq",
        split_axis=0,
        concat_axis=0,
        tiled=True,
    )
    slot_base = jnp.arange(per_peer, dtype=jnp.int32)[:, None] * seq_count
    landing = (
        run_starts[None, :] + slot_base + (seq_index - run_starts[None, :]) % seq_count
    ) // seq_count
    text_rows = text_embeds.shape[0]
    prompt = text_embeds.reshape(text_rows, D).at[landing.T.reshape(-1)].set(received.reshape(-1, D))
    text_normed = root_norm(prompt).astype(jnp.bfloat16)
    head_queries = root_norm(
        jnp.einsum(
            "td,dhe->hte",
            text_normed,
            decoder_q.reshape(D, local_heads, HEAD),
            preferred_element_type=jnp.float32,
        )
    ).astype(jnp.bfloat16)
    received_kv = key_value(received.reshape(-1, D))
    key_rows = text_kv[0].at[landing.T.reshape(-1)].set(received_kv[0])
    value_rows = text_kv[1].at[landing.T.reshape(-1)].set(received_kv[1])

    shared = jnp.stack([key_rows, value_rows], 0)[None]
    piece = lax.all_gather(shared, "seq", axis=0, tiled=True)
    rows = 64
    doc_starts = jnp.sum(
        (segment_ids[None] < jnp.arange(4, dtype=jnp.int32)[:, None, None]).astype(jnp.int32),
        (1, 2),
    )
    info = jnp.concatenate(
        [doc_starts, jnp.full((1,), seq_index, jnp.int32), jnp.zeros((3,), jnp.int32)]
    )
    decoder_out_full, head_queries = lax.optimization_barrier(
        (in_head_order(first, decoder_out, decoder_out_other, 0), head_queries)
    )
    head_major = text_attention(info, head_queries, piece, rows, scale)
    attended_text = jnp.transpose(head_major, (1, 0, 2)).reshape(text_rows, -1)
    all_heads = in_head_order(first, attended_text, swap(attended_text), 1)
    output_terms = jnp.dot(all_heads, decoder_out_full, preferred_element_type=jnp.float32)
    decoded = (prompt.astype(jnp.float32) + output_terms).astype(jnp.bfloat16)
    return decoded.reshape(text_rows, 1, D)


def solution(mesh):
    placed = (
        P("seq", None),
        P("seq", None),
        P("seq"),
        P(),
        P(None, "seq", None),
        P(),
        P(None, None, "section"),
        P("section", None),
        P("section", None, None),
        P(None, "section"),
        P(None, None, "section"),
        P("section", None),
    )
    return jax.shard_map(
        body, mesh=mesh, in_specs=placed, out_specs=P(None, "seq", None), check_vma=False
    )
```
